32 devices in a mesh: freq: 4 (over y, x), rblk: 8 (over z, core).
Axes of the slice: x: 2, y: 2, z: 4, core: 2. Of those that a mesh axis runs over, the one named last changes fastest.
Arguments:
- response: bfloat16 [8, 2, 64, 49, 128, 128], P('freq', None, 'rblk'), as said below
- aperture: int32 [64, 49], replicated, may hold values from -1 to 63, as said below
- focus_init: bfloat16 [8, 2, 4, 8192], P('freq', None, None, 'rblk'), may hold values from -6 to 6
- arrival: int32 [4, 8192], P(None, 'rblk'), may hold values from 512 to 3583
Outputs:
- focus_plus: bfloat16 [8, 2, 4, 8192], P('freq', None, None, 'rblk')
- focus_minus: bfloat16 [8, 2, 4, 8192], P('freq', None, None, 'rblk')
The draws below stay inside these ranges and needn't reach their ends.
Inputs may be any that keep to these rules, and one draw needn't show every extreme that they name: `aperture`: row b lists, in rising order, the source blocks that receiver block b needs, then -1 in its other slots. Blocks lie on a 8 x 8 grid: block b sits in grid row 2 * ((b % h) // 8) + b // h and grid column b % 8, with h half of 64. A block lists itself and only blocks at most 3 apart along each grid direction; b lists c exactly when c lists b; some block lists 49 blocks. response[:, :, b, j] is the block of R for receivers of block b and sources of block aperture[b, j]; slots with -1 hold values that are not part of R. Reciprocity: that block is the transpose of the block stored for receivers of block aperture[b, j] and sources of block b.
All inputs are finite; a program needn't handle non-finite values.
Results may differ from the reference program's by a relative error of at most 0.005.
Values may be sent and summed in bfloat16 or wider, within the bound.
No kernel may reach another device: no remote copies, remote signals or barrier semaphores. Data moves between devices by JAX's collectives and lax.ppermute only.
A program may use at most 192 MiB of HBM per device.

```python
import math
import jax
import jax.numpy as jnp
from jax import lax

NT = 4096
FBASE = 256
FREQ = 8
FOC = 4
BS = 128
NBLK = 64
GRID = 8
RAD = 3
APER = 49
NR = 8192
ITERS = 1


def aperture_table(key):
    base_key = jax.random.fold_in(key, 11)
    coin_key, row_key, col_key = jax.random.split(base_key, 3)
    blocks = jnp.arange(NBLK, dtype=jnp.int32)
    half_count = NBLK // 2
    grid_row = 2 * (blocks % half_count // GRID) + blocks // half_count
    grid_col = blocks % GRID
    distance = jnp.maximum(jnp.abs(grid_row[:, None] - grid_row[None, :]), jnp.abs(grid_col[:, None] - grid_col[None, :]))
    coins = jax.random.randint(coin_key, (NBLK, NBLK), 0, 2, dtype=jnp.int32)
    lower = jnp.minimum(blocks[:, None], blocks[None, :])
    upper = jnp.maximum(blocks[:, None], blocks[None, :])
    paired = coins[lower, upper]
    center_row = jax.random.randint(row_key, (), RAD, GRID - RAD, dtype=jnp.int32)
    center_col = jax.random.randint(col_key, (), RAD, GRID - RAD, dtype=jnp.int32)
    center = center_row % 2 * half_count + center_row // 2 * GRID + center_col
    listed = (distance <= RAD) & ((paired == 1) | (blocks[:, None] == blocks[None, :]) | (blocks[:, None] == center) | (blocks[None, :] == center))
    scores = jnp.where(listed, blocks[None, :], NBLK + blocks[None, :])
    ordered = jnp.sort(scores, axis=1)[:, :APER]
    return jnp.where(ordered < NBLK, ordered, -1).astype(jnp.int32)


def draw_aperture(key, part):
    return aperture_table(key)


def draw_response(key, part):
    table = aperture_table(key)
    scale = (2.0 * APER * BS) ** (-0.5)
    noise_key = jax.random.fold_in(key, 29)
    block_ids = jnp.repeat(jnp.arange(NBLK, dtype=jnp.int32), APER)
    slot_ids = jnp.tile(jnp.arange(APER, dtype=jnp.int32), NBLK)

    def one_tile(plane_key, block_id, slot_id):
        source = table[block_id, slot_id]
        lower = jnp.minimum(block_id, source)
        upper = jnp.maximum(block_id, source)
        pair_id = jnp.where(source < 0, NBLK * NBLK + block_id * APER + slot_id, lower * NBLK + upper)
        tile_key = jax.random.fold_in(plane_key, pair_id)
        values = jax.random.normal(tile_key, (BS, BS), jnp.float32)
        mirrored = jnp.where(block_id > source, values.T, values)
        values = jnp.where(block_id == source, (values + values.T) * math.sqrt(0.5), mirrored)
        return (values * scale).astype(jnp.bfloat16)

    def one_plane(plane_id):
        plane_key = jax.random.fold_in(noise_key, plane_id)
        return jax.vmap(lambda block_id, slot_id: one_tile(plane_key, block_id, slot_id))(block_ids, slot_ids)
    planes = lax.map(one_plane, jnp.arange(FREQ * 2, dtype=jnp.int32))
    return planes.reshape(FREQ, 2, NBLK, APER, BS, BS)


def touch_ends(result, stream_key, smallest, top_value):
    spot = [jax.random.randint(jax.random.fold_in(stream_key, axis), (), 0, length) for axis, length in enumerate(result.shape)]
    longest = result.shape.index(max(result.shape))
    neighbour = spot[:longest] + [(spot[longest] + 1) % result.shape[longest]] + spot[longest + 1:]
    return result.at[tuple(spot)].set(smallest).at[tuple(neighbour)].set(top_value)


def block_levels(key, extent, shards, low, largest):
    level = 1.0
    for dim, parts in shards:
        draws = jax.random.uniform(jax.random.fold_in(jax.random.fold_in(key, 6), dim), (parts,), jnp.float32, low / len(shards), largest / len(shards))
        level = level * jnp.repeat(jnp.exp(draws), extent[dim] // parts).reshape((-1,) + (1,) * (len(extent) - 1 - dim))
    return level


def noise(key, extent, width, limit, shards=(), held_as=jnp.bfloat16):
    values = jax.random.normal(key, extent, jnp.float32) * width
    if len(shards) > 0:
        values = block_levels(key, extent, shards, -0.22, 0.18) * values
    return jnp.clip(values, min=-limit, max=limit).astype(held_as)


def setup_inputs(seed: int = 0) -> dict:
    key_list = jax.random.split(jax.random.key(seed), 5)
    return {
        "response": draw_response(jax.random.fold_in(key_list[4], 71), 0),
        "aperture": draw_aperture(jax.random.fold_in(key_list[4], 71), 0),
        "focus_init": noise(key_list[2], (FREQ, 2, FOC, NR), 1.0, 6.0, ((0, 4), (3, 8))),
        "arrival": touch_ends(jax.random.randint(key_list[3], (FOC, NR), NT // 8, 7 * NT // 8), jax.random.fold_in(key_list[3], 1), NT // 8, (7 * NT // 8) - 1).astype(jnp.int32),
    }


highest = lax.Precision.HIGHEST


def dirichlet(offsets, arrival_block):
    span = 2 * NT
    limits = arrival_block[..., None, None]
    full_turn = (limits * offsets) % span
    half_turn = ((limits - 1) * offsets) % span
    base_turn = offsets % span
    is_zero = (offsets % NT) == 0
    denom = jnp.where(is_zero, jnp.float32(1.0), jnp.sin(jnp.float32(math.pi) * base_turn.astype(jnp.float32) / NT))
    ratio = jnp.where(is_zero, limits.astype(jnp.float32), jnp.sin(jnp.float32(math.pi) * full_turn.astype(jnp.float32) / NT) / denom)
    angle = jnp.float32(math.pi) * half_turn.astype(jnp.float32) / NT
    return ratio * jnp.cos(angle), ratio * jnp.sin(angle)


def window_ref(spectra, arrival):
    freqs = FBASE + jnp.arange(FREQ, dtype=jnp.int32)
    differ = freqs[:, None] - freqs[None, :]
    summed = -(freqs[:, None] + freqs[None, :])

    def one_block(index):
        start = (index * BS).astype(jnp.int32)
        spectra_block = lax.dynamic_slice_in_dim(spectra, start, BS, 3).astype(jnp.float32)
        arrival_block = lax.dynamic_slice_in_dim(arrival, start, BS, 1)
        near_re, near_im = dirichlet(differ, arrival_block)
        far_re, far_im = dirichlet(summed, arrival_block)
        real_in = spectra_block[:, 0]
        imag_in = spectra_block[:, 1]
        new_real = jnp.einsum("jqt,qtjl->lqt", real_in, near_re + far_re, precision=highest)
        new_real = new_real + jnp.einsum("jqt,qtjl->lqt", imag_in, far_im - near_im, precision=highest)
        new_imag = jnp.einsum("jqt,qtjl->lqt", real_in, near_im + far_im, precision=highest)
        new_imag = new_imag + jnp.einsum("jqt,qtjl->lqt", imag_in, near_re - far_re, precision=highest)
        return jnp.stack([new_real, new_imag], axis=1) / NT

    per_block = lax.map(one_block, jnp.arange(NBLK, dtype=jnp.int32))
    joined = jnp.transpose(per_block, (1, 2, 3, 0, 4)).reshape(FREQ, 2, FOC, NR)
    return joined.astype(jnp.bfloat16)


def forward_ref(focus, response, aperture):
    columns = focus.reshape(FREQ, 2, FOC, NBLK, BS)
    group_size = 2 * RAD + 1

    def one_block(index):
        aperture_row = aperture[index]
        live_count = jnp.sum((aperture_row >= 0).astype(jnp.int32))
        turn_count = (live_count + group_size - 1) // group_size
        tile_all = lax.dynamic_index_in_dim(response, index, 2, keepdims=False)

        def step(turn_index, running):
            slot_ids = turn_index * group_size + jnp.arange(group_size, dtype=jnp.int32)
            chosen = lax.dynamic_slice_in_dim(aperture_row, turn_index * group_size, group_size)
            is_valid = slot_ids < live_count
            safe_ids = jnp.where(is_valid, chosen, 0)
            pieces = jnp.take(columns, safe_ids, axis=3).astype(jnp.float32)
            pieces = jnp.where(is_valid[None, None, None, :, None], pieces, jnp.float32(0.0))
            tile_set = lax.dynamic_slice_in_dim(tile_all, turn_index * group_size, group_size, 2).astype(jnp.float32)
            products = jnp.einsum("fcqgs,fdgrs->fcdqr", pieces, tile_set, precision=highest)
            real_part = products[:, 0, 0] - products[:, 1, 1]
            imag_part = products[:, 1, 0] + products[:, 0, 1]
            return running + jnp.stack([real_part, imag_part], axis=1)

        return lax.fori_loop(0, turn_count, step, jnp.zeros((FREQ, 2, FOC, BS), jnp.float32))

    per_block = lax.map(one_block, jnp.arange(NBLK, dtype=jnp.int32))
    return jnp.transpose(per_block, (1, 2, 3, 0, 4)).reshape(FREQ, 2, FOC, NR)


def adjoint_ref(window_q, response, aperture):
    group_size = 2 * RAD + 1
    received_all = window_q.reshape(FREQ, 2, FOC, NBLK, BS)

    def one_block(buffer, index):
        aperture_row = aperture[index]
        live_count = jnp.sum((aperture_row >= 0).astype(jnp.int32))
        turn_count = (live_count + group_size - 1) // group_size
        tile_all = lax.dynamic_index_in_dim(response, index, 2, keepdims=False)
        received = lax.dynamic_index_in_dim(received_all, index, 3, keepdims=False).astype(jnp.float32)

        def step(turn_index, running):
            slot_ids = turn_index * group_size + jnp.arange(group_size, dtype=jnp.int32)
            chosen = lax.dynamic_slice_in_dim(aperture_row, turn_index * group_size, group_size)
            is_valid = slot_ids < live_count
            safe_ids = jnp.where(is_valid, chosen, 0)
            tile_set = lax.dynamic_slice_in_dim(tile_all, turn_index * group_size, group_size, 2).astype(jnp.float32)
            products = jnp.einsum("fcqr,fdgrs->fcdgqs", received, tile_set, precision=highest)
            real_part = products[:, 0, 0] + products[:, 1, 1]
            imag_part = products[:, 1, 0] - products[:, 0, 1]
            term = jnp.stack([real_part, imag_part], axis=1)
            term = jnp.where(is_valid[None, None, :, None, None], term, jnp.float32(0.0))
            term = jnp.transpose(term, (0, 1, 3, 2, 4))
            return running.at[:, :, :, safe_ids, :].add(term)

        return lax.fori_loop(0, turn_count, step, buffer), None

    start = jnp.zeros((FREQ, 2, FOC, NBLK, BS), jnp.float32)
    buffer, unused = lax.scan(one_block, start, jnp.arange(NBLK, dtype=jnp.int32))
    return buffer.reshape(FREQ, 2, FOC, NR)


def reference(response, aperture, focus_init, arrival):
    current = focus_init
    window_q = focus_init
    for iteration in range(ITERS):
        forward = forward_ref(current, response, aperture).astype(jnp.bfloat16)
        window_q = window_ref(forward, arrival)
        adjoint = adjoint_ref(window_q, response, aperture).astype(jnp.bfloat16)
        windowed = window_ref(adjoint, arrival)
        current = (focus_init.astype(jnp.float32) + windowed.astype(jnp.float32)).astype(jnp.bfloat16)
    return current, window_q
```

```python
import math

import jax
import jax.numpy as jnp
from jax import lax
from jax.experimental import pallas as pl
from jax.experimental.pallas import tpu as pltpu
from jax.sharding import PartitionSpec as P

NT = 4096
FBASE = 256
ITERS = 1
NBUF = 3


def chunk_width(aper_w):
    for width in range(min(8, aper_w), 0, -1):
        if aper_w % width == 0:
            return width
    return 1


def chunk_schedule(aperture, first_block, blk_dev, chunk):
    aper_w = aperture.shape[1]
    per_blk = aper_w // chunk
    rows = lax.dynamic_slice_in_dim(aperture, first_block, blk_dev, 0)
    live = jnp.sum((rows >= 0).astype(jnp.int32), axis=1)
    counts = (live + chunk - 1) // chunk
    ends = jnp.cumsum(counts)
    starts = ends - counts
    entry = jnp.arange(blk_dev * per_blk, dtype=jnp.int32)
    blocks = jnp.sum((ends[None, :] <= entry[:, None]).astype(jnp.int32), axis=1)
    blocks = jnp.minimum(blocks, blk_dev - 1)
    chunks = jnp.clip(entry - starts[blocks], 0, per_blk - 1)
    meta = jnp.stack([first_block.astype(jnp.int32), ends[-1]])
    return blocks, chunks, meta, live


def block_products(gathered, response, aperture, first_block, conjugate):
    freq_dev, unused, blk_dev, aper_w, block_rows, block_cols = response.shape
    rows_g = gathered.shape[2]
    chunk = chunk_width(aper_w)
    blocks, chunks, meta, live = chunk_schedule(aperture, first_block, blk_dev, chunk)
    flat_aperture = aperture.reshape(-1)
    focal = rows_g // 2

    def kernel(aper_ref, blk_ref, chk_ref, meta_ref, live_ref, resp_hbm, g_ref, out_ref,
               buf, sem, acc):
        first = meta_ref[0]
        total = meta_ref[1]
        acc[...] = jnp.zeros(acc.shape, jnp.float32)

        def start(entry, slot):
            b = blk_ref[entry]
            c = chk_ref[entry]
            pltpu.make_async_copy(
                resp_hbm.at[:, :, b, pl.ds(c * chunk, chunk)], buf.at[slot], sem.at[slot]
            ).start()

        for slot in range(NBUF):
            @pl.when(slot < total)
            def _():
                start(slot, slot)

        def body(entry, carry):
            slot = entry % NBUF
            b = blk_ref[entry]
            c = chk_ref[entry]
            pltpu.make_async_copy(
                resp_hbm.at[:, :, 0, pl.ds(0, chunk)], buf.at[slot], sem.at[slot]
            ).wait()
            count = live_ref[b]
            row = first + b
            for t in range(chunk):
                j = c * chunk + t

                @pl.when(j < count)
                def _():
                    src = aper_ref[row * aper_w + j]
                    for f in range(freq_dev):
                        piece = g_ref[src, f]
                        tile = buf[slot, f, :, t].reshape(2 * block_rows, block_cols)
                        acc[b, f] += lax.dot_general(
                            piece, tile, (((1,), (1,)), ((), ())),
                            preferred_element_type=jnp.float32,
                        )

            @pl.when(entry + NBUF < total)
            def _():
                start(entry + NBUF, slot)

            return carry

        lax.fori_loop(0, total, body, 0)

        for b in range(blk_dev):
            for f in range(freq_dev):
                v = acc[b, f]
                p00 = v[0:focal, 0:block_rows]
                p01 = v[0:focal, block_rows:]
                p10 = v[focal:, 0:block_rows]
                p11 = v[focal:, block_rows:]
                if conjugate:
                    real_part = p00 + p11
                    imag_part = p10 - p01
                else:
                    real_part = p00 - p11
                    imag_part = p10 + p01
                cols = pl.ds(b * block_rows, block_rows)
                out_ref[f, 0, :, cols] = real_part.astype(out_ref.dtype)
                out_ref[f, 1, :, cols] = imag_part.astype(out_ref.dtype)

    smem = pl.BlockSpec(memory_space=pltpu.SMEM)
    vmem = pl.BlockSpec(memory_space=pltpu.VMEM)
    return pl.pallas_call(
        kernel,
        out_shape=jax.ShapeDtypeStruct(
            (freq_dev, 2, focal, blk_dev * block_rows), jnp.bfloat16
        ),
        in_specs=[smem, smem, smem, smem, smem, pl.BlockSpec(memory_space=pl.ANY), vmem],
        out_specs=vmem,
        scratch_shapes=[
            pltpu.VMEM((NBUF, freq_dev, 2, chunk, block_rows, block_cols), response.dtype),
            pltpu.SemaphoreType.DMA((NBUF,)),
            pltpu.VMEM((blk_dev, freq_dev, rows_g, 2 * block_rows), jnp.float32),
        ],
    )(flat_aperture, blocks, chunks, meta, live, response, gathered)


def gather_columns(spectra, block_rows):
    freq_dev, unused, focal, traces = spectra.shape
    blk_dev = traces // block_rows
    local = spectra.reshape(freq_dev, 2 * focal, blk_dev, block_rows)
    local = jnp.transpose(local, (2, 0, 1, 3))
    return lax.all_gather(local, "rblk", axis=0, tiled=True)


def dirichlet(offsets, limits):
    span = 2 * NT
    full_turn = (limits * offsets) % span
    half_turn = ((limits - 1) * offsets) % span
    base_turn = offsets % span
    is_zero = (offsets % NT) == 0
    denom = jnp.where(
        is_zero, jnp.float32(1.0), jnp.sin(jnp.float32(math.pi) * base_turn.astype(jnp.float32) / NT)
    )
    ratio = jnp.where(
        is_zero,
        limits.astype(jnp.float32),
        jnp.sin(jnp.float32(math.pi) * full_turn.astype(jnp.float32) / NT) / denom,
    )
    angle = jnp.float32(math.pi) * half_turn.astype(jnp.float32) / NT
    return ratio * jnp.cos(angle), ratio * jnp.sin(angle)


def window_tables(arrival, freq_dev, freq_all):
    first = lax.axis_index("freq") * freq_dev
    mine = FBASE + first + jnp.arange(freq_dev, dtype=jnp.int32)
    every = FBASE + jnp.arange(freq_all, dtype=jnp.int32)
    limits = arrival[None, None]
    near_re, near_im = dirichlet((mine[:, None] - every[None, :])[:, :, None, None], limits)
    far_re, far_im = dirichlet((-(mine[:, None] + every[None, :]))[:, :, None, None], limits)
    scale = jnp.float32(1.0 / NT)
    return (
        (near_re + far_re) * scale,
        (far_im - near_im) * scale,
        (near_im + far_im) * scale,
        (near_re - far_re) * scale,
    )


def apply_window(spectra, tables):
    c_rr, c_ir, c_ri, c_ii = tables
    values = spectra.astype(jnp.float32)
    real_in = values[:, 0][:, None]
    imag_in = values[:, 1][:, None]
    new_real = jnp.sum(real_in * c_rr + imag_in * c_ir, axis=0)
    new_imag = jnp.sum(real_in * c_ri + imag_in * c_ii, axis=0)
    partial = jnp.stack([new_real, new_imag], axis=1)
    summed = lax.psum_scatter(partial, "freq", scatter_dimension=0, tiled=True)
    return summed.astype(jnp.bfloat16)


def shards(response, aperture, focus_init, arrival):
    freq_dev = response.shape[0]
    blk_dev = response.shape[2]
    block_rows = response.shape[4]
    freq_all = freq_dev * lax.axis_size("freq")
    first_block = lax.axis_index("rblk") * blk_dev
    tables = window_tables(arrival, freq_dev, freq_all)
    current = focus_init
    window_q = focus_init
    for iteration in range(ITERS):
        gathered = gather_columns(current, block_rows)
        forward = block_products(gathered, response, aperture, first_block, False)
        window_q = apply_window(forward, tables)
        mirrored = gather_columns(window_q, block_rows)
        adjoint = block_products(mirrored, response, aperture, first_block, True)
        windowed = apply_window(adjoint, tables)
        current = (focus_init.astype(jnp.float32) + windowed.astype(jnp.float32)).astype(
            jnp.bfloat16
        )
    return (current, window_q)


def solution(mesh):
    return jax.shard_map(
        shards,
        mesh=mesh,
        in_specs=(
            P("freq", None, "rblk", None, None, None),
            P(),
            P("freq", None, None, "rblk"),
            P(None, "rblk"),
        ),
        out_specs=(P("freq", None, None, "rblk"), P("freq", None, None, "rblk")),
        check_vma=False,
    )
```

```python
import math

import jax
import jax.numpy as jnp
from jax import lax
from jax.experimental import pallas as pl
from jax.experimental.pallas import tpu as pltpu
from jax.sharding import PartitionSpec as P

NT = 4096
FBASE = 256
ITERS = 1
NBUF = 3


def chunk_width(aper_w):
    for width in range(min(8, aper_w), 0, -1):
        if aper_w % width == 0:
            return width
    return 1


def chunk_schedule(aperture, first_block, blk_dev, chunk):
    aper_w = aperture.shape[1]
    per_blk = aper_w // chunk
    rows = lax.dynamic_slice_in_dim(aperture, first_block, blk_dev, 0)
    live = jnp.sum((rows >= 0).astype(jnp.int32), axis=1)
    counts = (live + chunk - 1) // chunk
    ends = jnp.cumsum(counts)
    starts = ends - counts
    entry = jnp.arange(blk_dev * per_blk, dtype=jnp.int32)
    blocks = jnp.sum((ends[None, :] <= entry[:, None]).astype(jnp.int32), axis=1)
    blocks = jnp.minimum(blocks, blk_dev - 1)
    chunks = jnp.clip(entry - starts[blocks], 0, per_blk - 1)
    meta = jnp.stack([first_block.astype(jnp.int32), ends[-1]])
    return blocks, chunks, meta, live


def block_products(gathered, response, aperture, first_block, conjugate):
    freq_dev, unused, blk_dev, aper_w, block_rows, block_cols = response.shape
    rows_g = gathered.shape[3]
    chunk = chunk_width(aper_w)
    blocks, chunks, meta, live = chunk_schedule(aperture, first_block, blk_dev, chunk)
    flat_aperture = aperture.reshape(-1)
    focal = rows_g // 2

    def kernel(aper_ref, blk_ref, chk_ref, meta_ref, live_ref, resp_hbm, g_ref, out_ref,
               buf, sem, pcat, acc):
        first = meta_ref[0]
        total = meta_ref[1]
        acc[...] = jnp.zeros(acc.shape, jnp.float32)

        def copies(entry, slot):
            b = blk_ref[entry]
            c = chk_ref[entry]
            return [
                pltpu.make_async_copy(
                    resp_hbm.at[:, :, b, c * chunk + t],
                    buf.at[slot, :, :, :, pl.ds(t * block_cols, block_cols)],
                    sem.at[slot, t],
                )
                for t in range(chunk)
            ]

        for slot in range(NBUF):
            @pl.when(slot < total)
            def _():
                for copy in copies(slot, slot):
                    copy.start()

        def body(entry, carry):
            slot = entry % NBUF
            b = blk_ref[entry]
            c = chk_ref[entry]
            count = live_ref[b]
            row = first + b
            for f in range(freq_dev):
                for t in range(chunk):
                    j = c * chunk + t
                    src = jnp.maximum(aper_ref[row * aper_w + j], 0)
                    piece = g_ref[src, f]
                    pcat[f, pl.ds(t * block_cols, block_cols), :] = jnp.where(
                        j < count, piece, jnp.zeros_like(piece)
                    )
            for copy in copies(entry, slot):
                copy.wait()
            for f in range(freq_dev):
                tiles = buf[slot, f].reshape(2 * block_rows, chunk * block_cols)
                acc[b, f] += jnp.dot(tiles, pcat[f], preferred_element_type=jnp.float32)

            @pl.when(entry + NBUF < total)
            def _():
                for copy in copies(entry + NBUF, slot):
                    copy.start()

            return carry

        lax.fori_loop(0, total, body, 0)

        for b in range(blk_dev):
            for f in range(freq_dev):
                v = acc[b, f].T
                p00 = v[0:focal, 0:block_rows]
                p01 = v[0:focal, block_rows:]
                p10 = v[focal:, 0:block_rows]
                p11 = v[focal:, block_rows:]
                if conjugate:
                    real_part = p00 + p11
                    imag_part = p10 - p01
                else:
                    real_part = p00 - p11
                    imag_part = p10 + p01
                cols = pl.ds(b * block_rows, block_rows)
                out_ref[f, 0, :, cols] = real_part.astype(out_ref.dtype)
                out_ref[f, 1, :, cols] = imag_part.astype(out_ref.dtype)

    smem = pl.BlockSpec(memory_space=pltpu.SMEM)
    vmem = pl.BlockSpec(memory_space=pltpu.VMEM)
    return pl.pallas_call(
        kernel,
        out_shape=jax.ShapeDtypeStruct(
            (freq_dev, 2, focal, blk_dev * block_rows), jnp.bfloat16
        ),
        in_specs=[smem, smem, smem, smem, smem, pl.BlockSpec(memory_space=pl.ANY), vmem],
        out_specs=vmem,
        scratch_shapes=[
            pltpu.VMEM((NBUF, freq_dev, 2, block_rows, chunk * block_cols), response.dtype),
            pltpu.SemaphoreType.DMA((NBUF, chunk)),
            pltpu.VMEM((freq_dev, chunk * block_cols, rows_g), response.dtype),
            pltpu.VMEM((blk_dev, freq_dev, 2 * block_rows, rows_g), jnp.float32),
        ],
    )(flat_aperture, blocks, chunks, meta, live, response, gathered)


def gather_columns(spectra, block_rows):
    freq_dev, unused, focal, traces = spectra.shape
    blk_dev = traces // block_rows
    local = spectra.reshape(freq_dev, 2 * focal, blk_dev, block_rows)
    local = jnp.transpose(local, (2, 0, 3, 1))
    return lax.all_gather(local, "rblk", axis=0, tiled=True)


def dirichlet(offsets, limits):
    span = 2 * NT
    full_turn = (limits * offsets) % span
    half_turn = ((limits - 1) * offsets) % span
    base_turn = offsets % span
    is_zero = (offsets % NT) == 0
    denom = jnp.where(
        is_zero, jnp.float32(1.0), jnp.sin(jnp.float32(math.pi) * base_turn.astype(jnp.float32) / NT)
    )
    ratio = jnp.where(
        is_zero,
        limits.astype(jnp.float32),
        jnp.sin(jnp.float32(math.pi) * full_turn.astype(jnp.float32) / NT) / denom,
    )
    angle = jnp.float32(math.pi) * half_turn.astype(jnp.float32) / NT
    return ratio * jnp.cos(angle), ratio * jnp.sin(angle)


def window_tables(arrival, freq_dev, freq_all):
    first = lax.axis_index("freq") * freq_dev
    mine = FBASE + first + jnp.arange(freq_dev, dtype=jnp.int32)
    every = FBASE + jnp.arange(freq_all, dtype=jnp.int32)
    limits = arrival[None, None]
    near_re, near_im = dirichlet((mine[:, None] - every[None, :])[:, :, None, None], limits)
    far_re, far_im = dirichlet((-(mine[:, None] + every[None, :]))[:, :, None, None], limits)
    scale = jnp.float32(1.0 / NT)
    return (
        (near_re + far_re) * scale,
        (far_im - near_im) * scale,
        (near_im + far_im) * scale,
        (near_re - far_re) * scale,
    )


def apply_window(spectra, tables):
    c_rr, c_ir, c_ri, c_ii = tables
    values = spectra.astype(jnp.float32)
    real_in = values[:, 0][:, None]
    imag_in = values[:, 1][:, None]
    new_real = jnp.sum(real_in * c_rr + imag_in * c_ir, axis=0)
    new_imag = jnp.sum(real_in * c_ri + imag_in * c_ii, axis=0)
    partial = jnp.stack([new_real, new_imag], axis=1)
    summed = lax.psum_scatter(partial, "freq", scatter_dimension=0, tiled=True)
    return summed.astype(jnp.bfloat16)


def shards(response, aperture, focus_init, arrival):
    freq_dev = response.shape[0]
    blk_dev = response.shape[2]
    block_rows = response.shape[4]
    freq_all = freq_dev * lax.axis_size("freq")
    first_block = lax.axis_index("rblk") * blk_dev
    tables = window_tables(arrival, freq_dev, freq_all)
    current = focus_init
    window_q = focus_init
    for iteration in range(ITERS):
        gathered = gather_columns(current, block_rows)
        forward = block_products(gathered, response, aperture, first_block, False)
        window_q = apply_window(forward, tables)
        mirrored = gather_columns(window_q, block_rows)
        adjoint = block_products(mirrored, response, aperture, first_block, True)
        windowed = apply_window(adjoint, tables)
        current = (focus_init.astype(jnp.float32) + windowed.astype(jnp.float32)).astype(
            jnp.bfloat16
        )
    return (current, window_q)


def solution(mesh):
    return jax.shard_map(
        shards,
        mesh=mesh,
        in_specs=(
            P("freq", None, "rblk", None, None, None),
            P(),
            P("freq", None, None, "rblk"),
            P(None, "rblk"),
        ),
        out_specs=(P("freq", None, None, "rblk"), P("freq", None, None, "rblk")),
        check_vma=False,
    )
```

```python
import math

import jax
import jax.numpy as jnp
from jax import lax
from jax.experimental import pallas as pl
from jax.experimental.pallas import tpu as pltpu
from jax.sharding import PartitionSpec as P

NT = 4096
FBASE = 256
ITERS = 1
NBUF = 3


def chunk_width(aper_w):
    for width in range(min(8, aper_w), 0, -1):
        if aper_w % width == 0:
            return width
    return 1


def chunk_schedule(aperture, first_block, blk_dev, chunk):
    aper_w = aperture.shape[1]
    per_blk = aper_w // chunk
    rows = lax.dynamic_slice_in_dim(aperture, first_block, blk_dev, 0)
    live = jnp.sum((rows >= 0).astype(jnp.int32), axis=1)
    counts = (live + chunk - 1) // chunk
    ends = jnp.cumsum(counts)
    starts = ends - counts
    entry = jnp.arange(blk_dev * per_blk, dtype=jnp.int32)
    blocks = jnp.sum((ends[None, :] <= entry[:, None]).astype(jnp.int32), axis=1)
    blocks = jnp.minimum(blocks, blk_dev - 1)
    chunks = jnp.clip(entry - starts[blocks], 0, per_blk - 1)
    meta = jnp.stack([first_block.astype(jnp.int32), ends[-1]])
    return blocks, chunks, meta, live


def block_products(gathered, response, aperture, first_block, conjugate):
    freq_dev, unused, blk_dev, aper_w, block_rows, block_cols = response.shape
    rows_g = gathered.shape[3]
    chunk = chunk_width(aper_w)
    blocks, chunks, meta, live = chunk_schedule(aperture, first_block, blk_dev, chunk)
    flat_aperture = aperture.reshape(-1)
    focal = rows_g // 2

    def kernel(aper_ref, blk_ref, chk_ref, meta_ref, live_ref, resp_hbm, g_ref, out_ref,
               buf, sem, pcat, acc):
        first = meta_ref[0]
        total = meta_ref[1]
        acc[...] = jnp.zeros(acc.shape, jnp.float32)

        def copies(entry, slot):
            b = blk_ref[entry]
            c = chk_ref[entry]
            return [
                pltpu.make_async_copy(
                    resp_hbm.at[:, :, b, c * chunk + t],
                    buf.at[slot, :, :, :, pl.ds(t * block_cols, block_cols)],
                    sem.at[slot, t],
                )
                for t in range(chunk)
            ]

        for slot in range(NBUF):
            @pl.when(slot < total)
            def _():
                for copy in copies(slot, slot):
                    copy.start()

        def body(entry, carry):
            slot = entry % NBUF
            b = blk_ref[entry]
            c = chk_ref[entry]
            count = live_ref[b]
            row = first + b
            for f in range(freq_dev):
                for t in range(chunk):
                    j = c * chunk + t
                    src = jnp.maximum(aper_ref[row * aper_w + j], 0)
                    piece = g_ref[src, f]
                    pcat[f, pl.ds(t * block_cols, block_cols), :] = jnp.where(
                        j < count, piece, jnp.zeros_like(piece)
                    )
            for copy in copies(entry, slot):
                copy.wait()
            for f in range(freq_dev):
                tiles = buf[slot, f].reshape(2 * block_rows, chunk * block_cols)
                acc[b, f] += jnp.dot(tiles, pcat[f], preferred_element_type=jnp.float32)

            @pl.when(entry + NBUF < total)
            def _():
                for copy in copies(entry + NBUF, slot):
                    copy.start()

            return carry

        lax.fori_loop(0, total, body, 0)

        for b in range(blk_dev):
            for f in range(freq_dev):
                v = acc[b, f].T
                p00 = v[0:focal, 0:block_rows]
                p01 = v[0:focal, block_rows:]
                p10 = v[focal:, 0:block_rows]
                p11 = v[focal:, block_rows:]
                if conjugate:
                    real_part = p00 + p11
                    imag_part = p10 - p01
                else:
                    real_part = p00 - p11
                    imag_part = p10 + p01
                cols = pl.ds(b * block_rows, block_rows)
                out_ref[f, 0, :, cols] = real_part.astype(out_ref.dtype)
                out_ref[f, 1, :, cols] = imag_part.astype(out_ref.dtype)

    smem = pl.BlockSpec(memory_space=pltpu.SMEM)
    vmem = pl.BlockSpec(memory_space=pltpu.VMEM)
    return pl.pallas_call(
        kernel,
        out_shape=jax.ShapeDtypeStruct(
            (freq_dev, 2, focal, blk_dev * block_rows), jnp.bfloat16
        ),
        in_specs=[smem, smem, smem, smem, smem, pl.BlockSpec(memory_space=pl.ANY), vmem],
        out_specs=vmem,
        scratch_shapes=[
            pltpu.VMEM((NBUF, freq_dev, 2, block_rows, chunk * block_cols), response.dtype),
            pltpu.SemaphoreType.DMA((NBUF, chunk)),
            pltpu.VMEM((freq_dev, chunk * block_cols, rows_g), response.dtype),
            pltpu.VMEM((blk_dev, freq_dev, 2 * block_rows, rows_g), jnp.float32),
        ],
    )(flat_aperture, blocks, chunks, meta, live, response, gathered)


def gather_columns(spectra, block_rows):
    freq_dev, unused, focal, traces = spectra.shape
    blk_dev = traces // block_rows
    local = spectra.reshape(freq_dev, 2 * focal, blk_dev, block_rows)
    local = jnp.transpose(local, (2, 0, 3, 1))
    return lax.all_gather(local, "rblk", axis=0, tiled=True)


def dirichlet(offsets, limits):
    span = 2 * NT
    full_turn = (limits * offsets) % span
    half_turn = ((limits - 1) * offsets) % span
    base_turn = offsets % span
    is_zero = (offsets % NT) == 0
    denom = jnp.where(
        is_zero, jnp.float32(1.0), jnp.sin(jnp.float32(math.pi) * base_turn.astype(jnp.float32) / NT)
    )
    ratio = jnp.where(
        is_zero,
        limits.astype(jnp.float32),
        jnp.sin(jnp.float32(math.pi) * full_turn.astype(jnp.float32) / NT) / denom,
    )
    angle = jnp.float32(math.pi) * half_turn.astype(jnp.float32) / NT
    return ratio * jnp.cos(angle), ratio * jnp.sin(angle)


def window_tables(arrival, freq_dev, freq_all):
    first = lax.axis_index("freq") * freq_dev
    mine = FBASE + first + jnp.arange(freq_dev, dtype=jnp.int32)
    every = FBASE + jnp.arange(freq_all, dtype=jnp.int32)
    limits = arrival[None, None]
    near_re, near_im = dirichlet((mine[:, None] - every[None, :])[:, :, None, None], limits)
    far_re, far_im = dirichlet((-(mine[:, None] + every[None, :]))[:, :, None, None], limits)
    scale = jnp.float32(1.0 / NT)
    return (
        (near_re + far_re) * scale,
        (far_im - near_im) * scale,
        (near_im + far_im) * scale,
        (near_re - far_re) * scale,
    )


def apply_window(spectra, tables):
    c_rr, c_ir, c_ri, c_ii = tables
    values = spectra.astype(jnp.float32)
    real_in = values[:, 0][:, None]
    imag_in = values[:, 1][:, None]
    new_real = jnp.sum(real_in * c_rr + imag_in * c_ir, axis=0)
    new_imag = jnp.sum(real_in * c_ri + imag_in * c_ii, axis=0)
    partial = jnp.stack([new_real, new_imag], axis=1)
    freq_dev = spectra.shape[0]
    count = lax.axis_size("freq")
    me = lax.axis_index("freq")
    summed = lax.dynamic_slice_in_dim(partial, me * freq_dev, freq_dev, 0)
    for shift in range(1, count):
        target = (me + shift) % count
        outgoing = lax.dynamic_slice_in_dim(partial, target * freq_dev, freq_dev, 0)
        pairs = [(i, (i + shift) % count) for i in range(count)]
        summed = summed + lax.ppermute(outgoing, "freq", pairs)
    return summed.astype(jnp.bfloat16)


def shards(response, aperture, focus_init, arrival):
    freq_dev = response.shape[0]
    blk_dev = response.shape[2]
    block_rows = response.shape[4]
    freq_all = freq_dev * lax.axis_size("freq")
    first_block = lax.axis_index("rblk") * blk_dev
    tables = window_tables(arrival, freq_dev, freq_all)
    current = focus_init
    window_q = focus_init
    for iteration in range(ITERS):
        gathered = gather_columns(current, block_rows)
        forward = block_products(gathered, response, aperture, first_block, False)
        window_q = apply_window(forward, tables)
        mirrored = gather_columns(window_q, block_rows)
        adjoint = block_products(mirrored, response, aperture, first_block, True)
        windowed = apply_window(adjoint, tables)
        current = (focus_init.astype(jnp.float32) + windowed.astype(jnp.float32)).astype(
            jnp.bfloat16
        )
    return (current, window_q)


def solution(mesh):
    return jax.shard_map(
        shards,
        mesh=mesh,
        in_specs=(
            P("freq", None, "rblk", None, None, None),
            P(),
            P("freq", None, None, "rblk"),
            P(None, "rblk"),
        ),
        out_specs=(P("freq", None, None, "rblk"), P("freq", None, None, "rblk")),
        check_vma=False,
    )
```

```python
import math

import jax
import jax.numpy as jnp
from jax import lax
from jax.experimental import pallas as pl
from jax.experimental.pallas import tpu as pltpu
from jax.sharding import PartitionSpec as P

NT = 4096
FBASE = 256
ITERS = 1
NBUF = 3


def chunk_width(aper_w):
    for width in range(min(8, aper_w), 0, -1):
        if aper_w % width == 0:
            return width
    return 1


def chunk_schedule(aperture, first_block, blk_dev, chunk):
    aper_w = aperture.shape[1]
    per_blk = aper_w // chunk
    rows = lax.dynamic_slice_in_dim(aperture, first_block, blk_dev, 0)
    live = jnp.sum((rows >= 0).astype(jnp.int32), axis=1)
    counts = (live + chunk - 1) // chunk
    ends = jnp.cumsum(counts)
    starts = ends - counts
    entry = jnp.arange(blk_dev * per_blk, dtype=jnp.int32)
    blocks = jnp.sum((ends[None, :] <= entry[:, None]).astype(jnp.int32), axis=1)
    blocks = jnp.minimum(blocks, blk_dev - 1)
    chunks = jnp.clip(entry - starts[blocks], 0, per_blk - 1)
    meta = jnp.stack([first_block.astype(jnp.int32), ends[-1]])
    return blocks, chunks, meta, live


def block_products(gathered, response, aperture, first_block, conjugate):
    freq_dev, unused, blk_dev, aper_w, block_rows, block_cols = response.shape
    rows_g = gathered.shape[2]
    chunk = chunk_width(aper_w)
    blocks, chunks, meta, live = chunk_schedule(aperture, first_block, blk_dev, chunk)
    flat_aperture = aperture.reshape(-1)
    focal = rows_g // 2

    def kernel(aper_ref, blk_ref, chk_ref, meta_ref, live_ref, resp_hbm, g_ref, out_ref,
               buf, sem, pcat, acc):
        first = meta_ref[0]
        total = meta_ref[1]
        acc[...] = jnp.zeros(acc.shape, jnp.float32)

        def copies(entry, slot):
            b = blk_ref[entry]
            c = chk_ref[entry]
            return [
                pltpu.make_async_copy(
                    resp_hbm.at[:, :, b, c * chunk + t],
                    buf.at[slot, :, :, :, pl.ds(t * block_cols, block_cols)],
                    sem.at[slot, t],
                )
                for t in range(chunk)
            ]

        for slot in range(NBUF):
            @pl.when(slot < total)
            def _():
                for copy in copies(slot, slot):
                    copy.start()

        def body(entry, carry):
            slot = entry % NBUF
            b = blk_ref[entry]
            c = chk_ref[entry]
            count = live_ref[b]
            row = first + b
            for f in range(freq_dev):
                for t in range(chunk):
                    j = c * chunk + t
                    src = jnp.maximum(aper_ref[row * aper_w + j], 0)
                    piece = g_ref[src, f]
                    pcat[f, :, pl.ds(t * block_cols, block_cols)] = jnp.where(
                        j < count, piece, jnp.zeros_like(piece)
                    )
            for copy in copies(entry, slot):
                copy.wait()
            for f in range(freq_dev):
                tiles = buf[slot, f].reshape(2 * block_rows, chunk * block_cols)
                acc[b, f] += lax.dot_general(
                    tiles, pcat[f], (((1,), (1,)), ((), ())),
                    preferred_element_type=jnp.float32,
                )

            @pl.when(entry + NBUF < total)
            def _():
                for copy in copies(entry + NBUF, slot):
                    copy.start()

            return carry

        lax.fori_loop(0, total, body, 0)

        for b in range(blk_dev):
            for f in range(freq_dev):
                v = acc[b, f].T
                p00 = v[0:focal, 0:block_rows]
                p01 = v[0:focal, block_rows:]
                p10 = v[focal:, 0:block_rows]
                p11 = v[focal:, block_rows:]
                if conjugate:
                    real_part = p00 + p11
                    imag_part = p10 - p01
                else:
                    real_part = p00 - p11
                    imag_part = p10 + p01
                cols = pl.ds(b * block_rows, block_rows)
                out_ref[f, 0, :, cols] = real_part.astype(out_ref.dtype)
                out_ref[f, 1, :, cols] = imag_part.astype(out_ref.dtype)

    smem = pl.BlockSpec(memory_space=pltpu.SMEM)
    vmem = pl.BlockSpec(memory_space=pltpu.VMEM)
    return pl.pallas_call(
        kernel,
        out_shape=jax.ShapeDtypeStruct(
            (freq_dev, 2, focal, blk_dev * block_rows), jnp.bfloat16
        ),
        in_specs=[smem, smem, smem, smem, smem, pl.BlockSpec(memory_space=pl.ANY), vmem],
        out_specs=vmem,
        scratch_shapes=[
            pltpu.VMEM((NBUF, freq_dev, 2, block_rows, chunk * block_cols), response.dtype),
            pltpu.SemaphoreType.DMA((NBUF, chunk)),
            pltpu.VMEM((freq_dev, rows_g, chunk * block_cols), response.dtype),
            pltpu.VMEM((blk_dev, freq_dev, 2 * block_rows, rows_g), jnp.float32),
        ],
    )(flat_aperture, blocks, chunks, meta, live, response, gathered)


def gather_columns(spectra, block_rows):
    freq_dev, unused, focal, traces = spectra.shape
    blk_dev = traces // block_rows
    local = spectra.reshape(freq_dev, 2 * focal, blk_dev, block_rows)
    local = jnp.transpose(local, (2, 0, 1, 3))
    count = lax.axis_size("rblk")
    if count & (count - 1):
        return lax.all_gather(local, "rblk", axis=0, tiled=True)
    step = 1
    while step < count:
        pairs = [(i, i ^ step) for i in range(count)]
        local = jnp.concatenate([local, lax.ppermute(local, "rblk", pairs)], axis=0)
        step *= 2
    return local


def arrival_order(aperture, blk_dev):
    count = lax.axis_size("rblk")
    if count & (count - 1):
        return aperture
    me = lax.axis_index("rblk")
    place = jnp.bitwise_xor(me, aperture // blk_dev)
    return jnp.where(aperture >= 0, place * blk_dev + aperture % blk_dev, aperture)


def dirichlet(offsets, limits):
    span = 2 * NT
    full_turn = (limits * offsets) % span
    half_turn = ((limits - 1) * offsets) % span
    base_turn = offsets % span
    is_zero = (offsets % NT) == 0
    denom = jnp.where(
        is_zero, jnp.float32(1.0), jnp.sin(jnp.float32(math.pi) * base_turn.astype(jnp.float32) / NT)
    )
    ratio = jnp.where(
        is_zero,
        limits.astype(jnp.float32),
        jnp.sin(jnp.float32(math.pi) * full_turn.astype(jnp.float32) / NT) / denom,
    )
    angle = jnp.float32(math.pi) * half_turn.astype(jnp.float32) / NT
    return ratio * jnp.cos(angle), ratio * jnp.sin(angle)


def window_tables(arrival, freq_dev, freq_all):
    first = lax.axis_index("freq") * freq_dev
    mine = FBASE + first + jnp.arange(freq_dev, dtype=jnp.int32)
    every = FBASE + jnp.arange(freq_all, dtype=jnp.int32)
    limits = arrival[None, None]
    near_re, near_im = dirichlet((mine[:, None] - every[None, :])[:, :, None, None], limits)
    far_re, far_im = dirichlet((-(mine[:, None] + every[None, :]))[:, :, None, None], limits)
    scale = jnp.float32(1.0 / NT)
    return (
        (near_re + far_re) * scale,
        (far_im - near_im) * scale,
        (near_im + far_im) * scale,
        (near_re - far_re) * scale,
    )


def apply_window(spectra, tables):
    c_rr, c_ir, c_ri, c_ii = tables
    values = spectra.astype(jnp.float32)
    real_in = values[:, 0][:, None]
    imag_in = values[:, 1][:, None]
    new_real = jnp.sum(real_in * c_rr + imag_in * c_ir, axis=0)
    new_imag = jnp.sum(real_in * c_ri + imag_in * c_ii, axis=0)
    partial = jnp.stack([new_real, new_imag], axis=1)
    freq_dev = spectra.shape[0]
    count = lax.axis_size("freq")
    me = lax.axis_index("freq")
    summed = lax.dynamic_slice_in_dim(partial, me * freq_dev, freq_dev, 0)
    for shift in range(1, count):
        target = (me + shift) % count
        outgoing = lax.dynamic_slice_in_dim(partial, target * freq_dev, freq_dev, 0)
        pairs = [(i, (i + shift) % count) for i in range(count)]
        summed = summed + lax.ppermute(outgoing, "freq", pairs)
    return summed.astype(jnp.bfloat16)


def shards(response, aperture, focus_init, arrival):
    freq_dev = response.shape[0]
    blk_dev = response.shape[2]
    block_rows = response.shape[4]
    freq_all = freq_dev * lax.axis_size("freq")
    first_block = lax.axis_index("rblk") * blk_dev
    tables = window_tables(arrival, freq_dev, freq_all)
    ordered = arrival_order(aperture, blk_dev)
    current = focus_init
    window_q = focus_init
    for iteration in range(ITERS):
        gathered = gather_columns(current, block_rows)
        forward = block_products(gathered, response, ordered, first_block, False)
        window_q = apply_window(forward, tables)
        mirrored = gather_columns(window_q, block_rows)
        adjoint = block_products(mirrored, response, ordered, first_block, True)
        windowed = apply_window(adjoint, tables)
        current = (focus_init.astype(jnp.float32) + windowed.astype(jnp.float32)).astype(
            jnp.bfloat16
        )
    return (current, window_q)


def solution(mesh):
    return jax.shard_map(
        shards,
        mesh=mesh,
        in_specs=(
            P("freq", None, "rblk", None, None, None),
            P(),
            P("freq", None, None, "rblk"),
            P(None, "rblk"),
        ),
        out_specs=(P("freq", None, None, "rblk"), P("freq", None, None, "rblk")),
        check_vma=False,
    )
```

```python
import math

import jax
import jax.numpy as jnp
from jax import lax
from jax.experimental import pallas as pl
from jax.experimental.pallas import tpu as pltpu
from jax.sharding import PartitionSpec as P

NT = 4096
FBASE = 256
ITERS = 1
NBUF = 5


def chunk_width(aper_w):
    for width in range(min(8, aper_w), 0, -1):
        if aper_w % width == 0:
            return width
    return 1


def chunk_schedule(aperture, first_block, blk_dev, chunk):
    aper_w = aperture.shape[1]
    per_blk = aper_w // chunk
    rows = lax.dynamic_slice_in_dim(aperture, first_block, blk_dev, 0)
    live = jnp.sum((rows >= 0).astype(jnp.int32), axis=1)
    counts = (live + chunk - 1) // chunk
    ends = jnp.cumsum(counts)
    starts = ends - counts
    entry = jnp.arange(blk_dev * per_blk, dtype=jnp.int32)
    blocks = jnp.sum((ends[None, :] <= entry[:, None]).astype(jnp.int32), axis=1)
    blocks = jnp.minimum(blocks, blk_dev - 1)
    chunks = jnp.clip(entry - starts[blocks], 0, per_blk - 1)
    meta = jnp.stack([first_block.astype(jnp.int32), ends[-1]])
    return blocks, chunks, meta, live


def block_products(gathered, response, aperture, first_block, conjugate):
    freq_dev, unused, blk_dev, aper_w, block_rows, block_cols = response.shape
    rows_g = gathered.shape[2]
    chunk = chunk_width(aper_w)
    blocks, chunks, meta, live = chunk_schedule(aperture, first_block, blk_dev, chunk)
    flat_aperture = aperture.reshape(-1)
    focal = rows_g // 2

    def kernel(aper_ref, blk_ref, chk_ref, meta_ref, live_ref, resp_hbm, g_ref, out_ref,
               buf, sem, pcat, acc):
        first = meta_ref[0]
        total = meta_ref[1]
        acc[...] = jnp.zeros(acc.shape, jnp.float32)

        def copies(entry, slot):
            b = blk_ref[entry]
            c = chk_ref[entry]
            return [
                pltpu.make_async_copy(
                    resp_hbm.at[:, :, b, c * chunk + t],
                    buf.at[slot, :, :, :, pl.ds(t * block_cols, block_cols)],
                    sem.at[slot, t],
                )
                for t in range(chunk)
            ]

        for slot in range(NBUF):
            @pl.when(slot < total)
            def _():
                for copy in copies(slot, slot):
                    copy.start()

        def body(entry, carry):
            slot = entry % NBUF
            b = blk_ref[entry]
            c = chk_ref[entry]
            count = live_ref[b]
            row = first + b
            for f in range(freq_dev):
                for t in range(chunk):
                    j = c * chunk + t
                    src = jnp.maximum(aper_ref[row * aper_w + j], 0)
                    piece = g_ref[src, f]
                    pcat[f, :, pl.ds(t * block_cols, block_cols)] = jnp.where(
                        j < count, piece, jnp.zeros_like(piece)
                    )
            for copy in copies(entry, slot):
                copy.wait()
            for f in range(freq_dev):
                tiles = buf[slot, f].reshape(2 * block_rows, chunk * block_cols)
                acc[b, f] += lax.dot_general(
                    tiles, pcat[f], (((1,), (1,)), ((), ())),
                    preferred_element_type=jnp.float32,
                )

            @pl.when(entry + NBUF < total)
            def _():
                for copy in copies(entry + NBUF, slot):
                    copy.start()

            return carry

        lax.fori_loop(0, total, body, 0)

        for b in range(blk_dev):
            for f in range(freq_dev):
                v = acc[b, f].T
                p00 = v[0:focal, 0:block_rows]
                p01 = v[0:focal, block_rows:]
                p10 = v[focal:, 0:block_rows]
                p11 = v[focal:, block_rows:]
                if conjugate:
                    real_part = p00 + p11
                    imag_part = p10 - p01
                else:
                    real_part = p00 - p11
                    imag_part = p10 + p01
                cols = pl.ds(b * block_rows, block_rows)
                out_ref[f, 0, :, cols] = real_part.astype(out_ref.dtype)
                out_ref[f, 1, :, cols] = imag_part.astype(out_ref.dtype)

    smem = pl.BlockSpec(memory_space=pltpu.SMEM)
    vmem = pl.BlockSpec(memory_space=pltpu.VMEM)
    return pl.pallas_call(
        kernel,
        out_shape=jax.ShapeDtypeStruct(
            (freq_dev, 2, focal, blk_dev * block_rows), jnp.bfloat16
        ),
        in_specs=[smem, smem, smem, smem, smem, pl.BlockSpec(memory_space=pl.ANY), vmem],
        out_specs=vmem,
        scratch_shapes=[
            pltpu.VMEM((NBUF, freq_dev, 2, block_rows, chunk * block_cols), response.dtype),
            pltpu.SemaphoreType.DMA((NBUF, chunk)),
            pltpu.VMEM((freq_dev, rows_g, chunk * block_cols), response.dtype),
            pltpu.VMEM((blk_dev, freq_dev, 2 * block_rows, rows_g), jnp.float32),
        ],
    )(flat_aperture, blocks, chunks, meta, live, response, gathered)


def gather_columns(spectra, block_rows):
    freq_dev, unused, focal, traces = spectra.shape
    blk_dev = traces // block_rows
    local = spectra.reshape(freq_dev, 2 * focal, blk_dev, block_rows)
    local = jnp.transpose(local, (2, 0, 1, 3))
    count = lax.axis_size("rblk")
    if count & (count - 1):
        return lax.all_gather(local, "rblk", axis=0, tiled=True)
    step = 1
    while step < count:
        pairs = [(i, i ^ step) for i in range(count)]
        local = jnp.concatenate([local, lax.ppermute(local, "rblk", pairs)], axis=0)
        step *= 2
    return local


def arrival_order(aperture, blk_dev):
    count = lax.axis_size("rblk")
    if count & (count - 1):
        return aperture
    me = lax.axis_index("rblk")
    place = jnp.bitwise_xor(me, aperture // blk_dev)
    return jnp.where(aperture >= 0, place * blk_dev + aperture % blk_dev, aperture)


def dirichlet(offsets, limits):
    span = 2 * NT
    full_turn = (limits * offsets) % span
    half_turn = ((limits - 1) * offsets) % span
    base_turn = offsets % span
    is_zero = (offsets % NT) == 0
    denom = jnp.where(
        is_zero, jnp.float32(1.0), jnp.sin(jnp.float32(math.pi) * base_turn.astype(jnp.float32) / NT)
    )
    ratio = jnp.where(
        is_zero,
        limits.astype(jnp.float32),
        jnp.sin(jnp.float32(math.pi) * full_turn.astype(jnp.float32) / NT) / denom,
    )
    angle = jnp.float32(math.pi) * half_turn.astype(jnp.float32) / NT
    return ratio * jnp.cos(angle), ratio * jnp.sin(angle)


def window_tables(arrival, freq_dev, freq_all):
    first = lax.axis_index("freq") * freq_dev
    mine = FBASE + first + jnp.arange(freq_dev, dtype=jnp.int32)
    every = FBASE + jnp.arange(freq_all, dtype=jnp.int32)
    limits = arrival[None, None]
    near_re, near_im = dirichlet((mine[:, None] - every[None, :])[:, :, None, None], limits)
    far_re, far_im = dirichlet((-(mine[:, None] + every[None, :]))[:, :, None, None], limits)
    scale = jnp.float32(1.0 / NT)
    return (
        (near_re + far_re) * scale,
        (far_im - near_im) * scale,
        (near_im + far_im) * scale,
        (near_re - far_re) * scale,
    )


def apply_window(spectra, tables):
    c_rr, c_ir, c_ri, c_ii = tables
    values = spectra.astype(jnp.float32)
    real_in = values[:, 0][:, None]
    imag_in = values[:, 1][:, None]
    new_real = jnp.sum(real_in * c_rr + imag_in * c_ir, axis=0)
    new_imag = jnp.sum(real_in * c_ri + imag_in * c_ii, axis=0)
    partial = jnp.stack([new_real, new_imag], axis=1)
    freq_dev = spectra.shape[0]
    count = lax.axis_size("freq")
    me = lax.axis_index("freq")
    summed = lax.dynamic_slice_in_dim(partial, me * freq_dev, freq_dev, 0)
    for shift in range(1, count):
        target = (me + shift) % count
        outgoing = lax.dynamic_slice_in_dim(partial, target * freq_dev, freq_dev, 0)
        pairs = [(i, (i + shift) % count) for i in range(count)]
        summed = summed + lax.ppermute(outgoing, "freq", pairs)
    return summed.astype(jnp.bfloat16)


def shards(response, aperture, focus_init, arrival):
    freq_dev = response.shape[0]
    blk_dev = response.shape[2]
    block_rows = response.shape[4]
    freq_all = freq_dev * lax.axis_size("freq")
    first_block = lax.axis_index("rblk") * blk_dev
    tables = window_tables(arrival, freq_dev, freq_all)
    ordered = arrival_order(aperture, blk_dev)
    current = focus_init
    window_q = focus_init
    for iteration in range(ITERS):
        gathered = gather_columns(current, block_rows)
        forward = block_products(gathered, response, ordered, first_block, False)
        window_q = apply_window(forward, tables)
        mirrored = gather_columns(window_q, block_rows)
        adjoint = block_products(mirrored, response, ordered, first_block, True)
        windowed = apply_window(adjoint, tables)
        current = (focus_init.astype(jnp.float32) + windowed.astype(jnp.float32)).astype(
            jnp.bfloat16
        )
    return (current, window_q)


def solution(mesh):
    return jax.shard_map(
        shards,
        mesh=mesh,
        in_specs=(
            P("freq", None, "rblk", None, None, None),
            P(),
            P("freq", None, None, "rblk"),
            P(None, "rblk"),
        ),
        out_specs=(P("freq", None, None, "rblk"), P("freq", None, None, "rblk")),
        check_vma=False,
    )
```

```python
import math

import jax
import jax.numpy as jnp
from jax import lax
from jax.experimental import pallas as pl
from jax.experimental.pallas import tpu as pltpu
from jax.sharding import PartitionSpec as P

NT = 4096
FBASE = 256
ITERS = 1
BLOCK = 128
NBUF = 5


def chunk_width(aper_w):
    for width in range(min(8, aper_w), 0, -1):
        if aper_w % width == 0:
            return width
    return 1


def chunk_schedule(aperture, first_block, blk_dev, chunk):
    aper_w = aperture.shape[1]
    per_blk = aper_w // chunk
    rows = lax.dynamic_slice_in_dim(aperture, first_block, blk_dev, 0)
    live = jnp.sum((rows >= 0).astype(jnp.int32), axis=1)
    counts = (live + chunk - 1) // chunk
    ends = jnp.cumsum(counts)
    starts = ends - counts
    entry = jnp.arange(blk_dev * per_blk, dtype=jnp.int32)
    blocks = jnp.sum((ends[None, :] <= entry[:, None]).astype(jnp.int32), axis=1)
    blocks = jnp.minimum(blocks, blk_dev - 1)
    chunks = jnp.clip(entry - starts[blocks], 0, per_blk - 1)
    meta = jnp.stack([first_block.astype(jnp.int32), ends[-1]])
    return blocks, chunks, meta, live


def block_products(gathered, response, aperture, first_block, tables, conjugate):
    freq_dev, unused, blk_dev, aper_w, block_rows, block_cols = response.shape
    rows_g = gathered.shape[2]
    chunk = chunk_width(aper_w)
    blocks, chunks, meta, live = chunk_schedule(aperture, first_block, blk_dev, chunk)
    flat_aperture = aperture.reshape(-1)
    focal = rows_g // 2
    freq_all = tables[0].shape[0] - freq_dev + 1
    scale = 1.0 / NT

    def kernel(aper_ref, blk_ref, chk_ref, meta_ref, live_ref, resp_hbm, g_ref,
               near_re_ref, near_im_ref, far_re_ref, far_im_ref, out_ref, buf, sem, pcat, acc):
        first = meta_ref[0]
        total = meta_ref[1]
        acc[...] = jnp.zeros(acc.shape, jnp.float32)

        def copies(entry, slot):
            b = blk_ref[entry]
            c = chk_ref[entry]
            return [
                pltpu.make_async_copy(
                    resp_hbm.at[:, :, b, c * chunk + t],
                    buf.at[slot, :, :, :, pl.ds(t * block_cols, block_cols)],
                    sem.at[slot, t],
                )
                for t in range(chunk)
            ]

        for slot in range(NBUF):
            @pl.when(slot < total)
            def _():
                for copy in copies(slot, slot):
                    copy.start()

        def body(entry, carry):
            slot = entry % NBUF
            b = blk_ref[entry]
            c = chk_ref[entry]
            count = live_ref[b]
            row = first + b
            for f in range(freq_dev):
                for t in range(chunk):
                    j = c * chunk + t
                    src = jnp.maximum(aper_ref[row * aper_w + j], 0)
                    piece = g_ref[src, f]
                    pcat[f, :, pl.ds(t * block_cols, block_cols)] = jnp.where(
                        j < count, piece, jnp.zeros_like(piece)
                    )
            for copy in copies(entry, slot):
                copy.wait()
            for f in range(freq_dev):
                tiles = buf[slot, f].reshape(2 * block_rows, chunk * block_cols)
                acc[b, f] += lax.dot_general(
                    tiles, pcat[f], (((1,), (1,)), ((), ())),
                    preferred_element_type=jnp.float32,
                )

            @pl.when(entry + NBUF < total)
            def _():
                for copy in copies(entry + NBUF, slot):
                    copy.start()

            return carry

        lax.fori_loop(0, total, body, 0)

        for b in range(blk_dev):
            cols = pl.ds(b * block_rows, block_rows)
            parts = []
            for f in range(freq_dev):
                v = acc[b, f].T
                p00 = v[0:focal, 0:block_rows]
                p01 = v[0:focal, block_rows:]
                p10 = v[focal:, 0:block_rows]
                p11 = v[focal:, block_rows:]
                if conjugate:
                    real_part = p00 + p11
                    imag_part = p10 - p01
                else:
                    real_part = p00 - p11
                    imag_part = p10 + p01
                parts.append((
                    real_part.astype(jnp.bfloat16).astype(jnp.float32),
                    imag_part.astype(jnp.bfloat16).astype(jnp.float32),
                ))
            for l in range(freq_all):
                new_real = None
                new_imag = None
                for f, (real_in, imag_in) in enumerate(parts):
                    near_at = f - l + freq_all - 1
                    far_at = f + l
                    rows = pl.ds(b * focal, focal)
                    near_re = near_re_ref[near_at, rows, :]
                    near_im = near_im_ref[near_at, rows, :]
                    far_re = far_re_ref[far_at, rows, :]
                    far_im = far_im_ref[far_at, rows, :]
                    term_real = real_in * (near_re + far_re) + imag_in * (far_im - near_im)
                    term_imag = real_in * (near_im + far_im) + imag_in * (near_re - far_re)
                    new_real = term_real if new_real is None else new_real + term_real
                    new_imag = term_imag if new_imag is None else new_imag + term_imag
                out_ref[l, 0, :, cols] = new_real * scale
                out_ref[l, 1, :, cols] = new_imag * scale

    smem = pl.BlockSpec(memory_space=pltpu.SMEM)
    vmem = pl.BlockSpec(memory_space=pltpu.VMEM)
    return pl.pallas_call(
        kernel,
        out_shape=jax.ShapeDtypeStruct(
            (freq_all, 2, focal, blk_dev * block_rows), jnp.float32
        ),
        in_specs=[smem] * 5 + [pl.BlockSpec(memory_space=pl.ANY)] + [vmem] * 5,
        out_specs=vmem,
        scratch_shapes=[
            pltpu.VMEM((NBUF, freq_dev, 2, block_rows, chunk * block_cols), response.dtype),
            pltpu.SemaphoreType.DMA((NBUF, chunk)),
            pltpu.VMEM((freq_dev, rows_g, chunk * block_cols), response.dtype),
            pltpu.VMEM((blk_dev, freq_dev, 2 * block_rows, rows_g), jnp.float32),
        ],
    )(flat_aperture, blocks, chunks, meta, live, response, gathered, *tables)


def gather_columns(spectra, block_rows):
    freq_dev, unused, focal, traces = spectra.shape
    blk_dev = traces // block_rows
    local = spectra.reshape(freq_dev, 2 * focal, blk_dev, block_rows)
    local = jnp.transpose(local, (2, 0, 1, 3))
    count = lax.axis_size("rblk")
    if count & (count - 1):
        return lax.all_gather(local, "rblk", axis=0, tiled=True)
    step = 1
    while step < count:
        pairs = [(i, i ^ step) for i in range(count)]
        local = jnp.concatenate([local, lax.ppermute(local, "rblk", pairs)], axis=0)
        step *= 2
    return local


def arrival_order(aperture, blk_dev):
    count = lax.axis_size("rblk")
    if count & (count - 1):
        return aperture
    me = lax.axis_index("rblk")
    place = jnp.bitwise_xor(me, aperture // blk_dev)
    return jnp.where(aperture >= 0, place * blk_dev + aperture % blk_dev, aperture)


def dirichlet(offsets, limits):
    span = 2 * NT
    full_turn = (limits * offsets) % span
    half_turn = ((limits - 1) * offsets) % span
    base_turn = offsets % span
    is_zero = (offsets % NT) == 0
    denom = jnp.where(
        is_zero, jnp.float32(1.0), jnp.sin(jnp.float32(math.pi) * base_turn.astype(jnp.float32) / NT)
    )
    ratio = jnp.where(
        is_zero,
        limits.astype(jnp.float32),
        jnp.sin(jnp.float32(math.pi) * full_turn.astype(jnp.float32) / NT) / denom,
    )
    angle = jnp.float32(math.pi) * half_turn.astype(jnp.float32) / NT
    return ratio * jnp.cos(angle), ratio * jnp.sin(angle)


def window_tables(arrival, freq_dev, freq_all):
    first = lax.axis_index("freq") * freq_dev
    steps = jnp.arange(freq_dev + freq_all - 1, dtype=jnp.int32)
    focal, traces = arrival.shape
    blocks = traces // BLOCK
    dense = jnp.transpose(arrival.reshape(focal, blocks, BLOCK), (1, 0, 2))
    limits = dense.reshape(blocks * focal, BLOCK)[None]
    near_offsets = first - (freq_all - 1) + steps
    far_offsets = -(2 * FBASE + first + steps)
    near_re, near_im = dirichlet(near_offsets[:, None, None], limits)
    far_re, far_im = dirichlet(far_offsets[:, None, None], limits)
    return near_re, near_im, far_re, far_im


def reduce_window(partial, freq_dev):
    count = lax.axis_size("freq")
    me = lax.axis_index("freq")
    summed = lax.dynamic_slice_in_dim(partial, me * freq_dev, freq_dev, 0)
    for shift in range(1, count):
        target = (me + shift) % count
        outgoing = lax.dynamic_slice_in_dim(partial, target * freq_dev, freq_dev, 0)
        pairs = [(i, (i + shift) % count) for i in range(count)]
        summed = summed + lax.ppermute(outgoing, "freq", pairs)
    return summed.astype(jnp.bfloat16)


def shards(response, aperture, focus_init, arrival):
    freq_dev = response.shape[0]
    blk_dev = response.shape[2]
    block_rows = response.shape[4]
    freq_all = freq_dev * lax.axis_size("freq")
    first_block = lax.axis_index("rblk") * blk_dev
    tables = window_tables(arrival, freq_dev, freq_all)
    ordered = arrival_order(aperture, blk_dev)
    current = focus_init
    window_q = focus_init
    for iteration in range(ITERS):
        gathered = gather_columns(current, block_rows)
        forward = block_products(gathered, response, ordered, first_block, tables, False)
        window_q = reduce_window(forward, freq_dev)
        mirrored = gather_columns(window_q, block_rows)
        adjoint = block_products(mirrored, response, ordered, first_block, tables, True)
        windowed = reduce_window(adjoint, freq_dev)
        current = (focus_init.astype(jnp.float32) + windowed.astype(jnp.float32)).astype(
            jnp.bfloat16
        )
    return (current, window_q)


def solution(mesh):
    return jax.shard_map(
        shards,
        mesh=mesh,
        in_specs=(
            P("freq", None, "rblk", None, None, None),
            P(),
            P("freq", None, None, "rblk"),
            P(None, "rblk"),
        ),
        out_specs=(P("freq", None, None, "rblk"), P("freq", None, None, "rblk")),
        check_vma=False,
    )
```

```python
import math

import jax
import jax.numpy as jnp
from jax import lax
from jax.experimental import pallas as pl
from jax.experimental.pallas import tpu as pltpu
from jax.sharding import PartitionSpec as P

NT = 4096
FBASE = 256
ITERS = 1
BLOCK = 128
NBUF = 5


def chunk_width(aper_w):
    for width in range(min(8, aper_w), 0, -1):
        if aper_w % width == 0:
            return width
    return 1


def live_counts(aperture, first_block, blk_dev):
    rows = lax.dynamic_slice_in_dim(aperture, first_block, blk_dev, 0)
    live = jnp.sum((rows >= 0).astype(jnp.int32), axis=1)
    return first_block.astype(jnp.int32).reshape(1), live


def block_products(gathered, response, aperture, first_block, tables, conjugate):
    freq_dev, unused, blk_dev, aper_w, block_rows, block_cols = response.shape
    rows_g = gathered.shape[2]
    chunk = chunk_width(aper_w)
    per_blk = aper_w // chunk
    meta, live = live_counts(aperture, first_block, blk_dev)
    flat_aperture = aperture.reshape(-1)
    focal = rows_g // 2
    freq_all = tables[0].shape[0] - freq_dev + 1
    scale = 1.0 / NT

    def kernel(aper_ref, meta_ref, live_ref, resp_hbm, g_ref,
               near_re_ref, near_im_ref, far_re_ref, far_im_ref, out_ref, buf, sem, pcat, acc,
               blk_ref, chk_ref):
        first = meta_ref[0]
        total = jnp.int32(0)
        for b in range(blk_dev):
            chunk_count = (live_ref[b] + chunk - 1) // chunk

            def fill(c, carry, b=b, base=total):
                blk_ref[base + c] = b
                chk_ref[base + c] = c
                return carry

            lax.fori_loop(0, chunk_count, fill, 0)
            total = total + chunk_count
        acc[...] = jnp.zeros(acc.shape, jnp.float32)

        def copies(entry, slot):
            b = blk_ref[entry]
            c = chk_ref[entry]
            return [
                pltpu.make_async_copy(
                    resp_hbm.at[:, :, b, c * chunk + t],
                    buf.at[slot, :, :, :, pl.ds(t * block_cols, block_cols)],
                    sem.at[slot, t],
                )
                for t in range(chunk)
            ]

        for slot in range(NBUF):
            @pl.when(slot < total)
            def _():
                for copy in copies(slot, slot):
                    copy.start()

        def body(entry, carry):
            slot = entry % NBUF
            b = blk_ref[entry]
            c = chk_ref[entry]
            count = live_ref[b]
            row = first + b
            for f in range(freq_dev):
                for t in range(chunk):
                    j = c * chunk + t
                    src = jnp.maximum(aper_ref[row * aper_w + j], 0)
                    piece = g_ref[src, f]
                    pcat[f, :, pl.ds(t * block_cols, block_cols)] = jnp.where(
                        j < count, piece, jnp.zeros_like(piece)
                    )
            for copy in copies(entry, slot):
                copy.wait()
            for f in range(freq_dev):
                tiles = buf[slot, f].reshape(2 * block_rows, chunk * block_cols)
                acc[b, f] += lax.dot_general(
                    tiles, pcat[f], (((1,), (1,)), ((), ())),
                    preferred_element_type=jnp.float32,
                )

            @pl.when(entry + NBUF < total)
            def _():
                for copy in copies(entry + NBUF, slot):
                    copy.start()

            return carry

        lax.fori_loop(0, total, body, 0)

        for b in range(blk_dev):
            cols = pl.ds(b * block_rows, block_rows)
            parts = []
            for f in range(freq_dev):
                v = acc[b, f].T
                p00 = v[0:focal, 0:block_rows]
                p01 = v[0:focal, block_rows:]
                p10 = v[focal:, 0:block_rows]
                p11 = v[focal:, block_rows:]
                if conjugate:
                    real_part = p00 + p11
                    imag_part = p10 - p01
                else:
                    real_part = p00 - p11
                    imag_part = p10 + p01
                parts.append((
                    real_part.astype(jnp.bfloat16).astype(jnp.float32),
                    imag_part.astype(jnp.bfloat16).astype(jnp.float32),
                ))
            for l in range(freq_all):
                new_real = None
                new_imag = None
                for f, (real_in, imag_in) in enumerate(parts):
                    near_at = f - l + freq_all - 1
                    far_at = f + l
                    rows = pl.ds(b * focal, focal)
                    near_re = near_re_ref[near_at, rows, :]
                    near_im = near_im_ref[near_at, rows, :]
                    far_re = far_re_ref[far_at, rows, :]
                    far_im = far_im_ref[far_at, rows, :]
                    term_real = real_in * (near_re + far_re) + imag_in * (far_im - near_im)
                    term_imag = real_in * (near_im + far_im) + imag_in * (near_re - far_re)
                    new_real = term_real if new_real is None else new_real + term_real
                    new_imag = term_imag if new_imag is None else new_imag + term_imag
                out_ref[l, 0, :, cols] = new_real * scale
                out_ref[l, 1, :, cols] = new_imag * scale

    smem = pl.BlockSpec(memory_space=pltpu.SMEM)
    vmem = pl.BlockSpec(memory_space=pltpu.VMEM)
    return pl.pallas_call(
        kernel,
        out_shape=jax.ShapeDtypeStruct(
            (freq_all, 2, focal, blk_dev * block_rows), jnp.float32
        ),
        in_specs=[smem] * 3 + [pl.BlockSpec(memory_space=pl.ANY)] + [vmem] * 5,
        out_specs=vmem,
        scratch_shapes=[
            pltpu.VMEM((NBUF, freq_dev, 2, block_rows, chunk * block_cols), response.dtype),
            pltpu.SemaphoreType.DMA((NBUF, chunk)),
            pltpu.VMEM((freq_dev, rows_g, chunk * block_cols), response.dtype),
            pltpu.VMEM((blk_dev, freq_dev, 2 * block_rows, rows_g), jnp.float32),
            pltpu.SMEM((blk_dev * per_blk,), jnp.int32),
            pltpu.SMEM((blk_dev * per_blk,), jnp.int32),
        ],
    )(flat_aperture, meta, live, response, gathered, *tables)


def gather_columns(spectra, block_rows):
    freq_dev, unused, focal, traces = spectra.shape
    blk_dev = traces // block_rows
    local = spectra.reshape(freq_dev, 2 * focal, blk_dev, block_rows)
    local = jnp.transpose(local, (2, 0, 1, 3))
    count = lax.axis_size("rblk")
    if count & (count - 1):
        return lax.all_gather(local, "rblk", axis=0, tiled=True)
    step = 1
    while step < count:
        pairs = [(i, i ^ step) for i in range(count)]
        local = jnp.concatenate([local, lax.ppermute(local, "rblk", pairs)], axis=0)
        step *= 2
    return local


def arrival_order(aperture, blk_dev):
    count = lax.axis_size("rblk")
    if count & (count - 1):
        return aperture
    me = lax.axis_index("rblk")
    place = jnp.bitwise_xor(me, aperture // blk_dev)
    return jnp.where(aperture >= 0, place * blk_dev + aperture % blk_dev, aperture)


def dirichlet(offsets, limits):
    span = 2 * NT
    full_turn = (limits * offsets) % span
    half_turn = ((limits - 1) * offsets) % span
    base_turn = offsets % span
    is_zero = (offsets % NT) == 0
    denom = jnp.where(
        is_zero, jnp.float32(1.0), jnp.sin(jnp.float32(math.pi) * base_turn.astype(jnp.float32) / NT)
    )
    ratio = jnp.where(
        is_zero,
        limits.astype(jnp.float32),
        jnp.sin(jnp.float32(math.pi) * full_turn.astype(jnp.float32) / NT) / denom,
    )
    angle = jnp.float32(math.pi) * half_turn.astype(jnp.float32) / NT
    return ratio * jnp.cos(angle), ratio * jnp.sin(angle)


def window_tables(arrival, freq_dev, freq_all):
    first = lax.axis_index("freq") * freq_dev
    steps = jnp.arange(freq_dev + freq_all - 1, dtype=jnp.int32)
    focal, traces = arrival.shape
    blocks = traces // BLOCK
    dense = jnp.transpose(arrival.reshape(focal, blocks, BLOCK), (1, 0, 2))
    limits = dense.reshape(blocks * focal, BLOCK)[None]
    near_offsets = first - (freq_all - 1) + steps
    far_offsets = -(2 * FBASE + first + steps)
    near_re, near_im = dirichlet(near_offsets[:, None, None], limits)
    far_re, far_im = dirichlet(far_offsets[:, None, None], limits)
    return near_re, near_im, far_re, far_im


def reduce_window(partial, freq_dev):
    count = lax.axis_size("freq")
    me = lax.axis_index("freq")
    summed = lax.dynamic_slice_in_dim(partial, me * freq_dev, freq_dev, 0)
    for shift in range(1, count):
        target = (me + shift) % count
        outgoing = lax.dynamic_slice_in_dim(partial, target * freq_dev, freq_dev, 0)
        pairs = [(i, (i + shift) % count) for i in range(count)]
        summed = summed + lax.ppermute(outgoing, "freq", pairs)
    return summed.astype(jnp.bfloat16)


def shards(response, aperture, focus_init, arrival):
    freq_dev = response.shape[0]
    blk_dev = response.shape[2]
    block_rows = response.shape[4]
    freq_all = freq_dev * lax.axis_size("freq")
    first_block = lax.axis_index("rblk") * blk_dev
    tables = window_tables(arrival, freq_dev, freq_all)
    ordered = arrival_order(aperture, blk_dev)
    current = focus_init
    window_q = focus_init
    for iteration in range(ITERS):
        gathered = gather_columns(current, block_rows)
        forward = block_products(gathered, response, ordered, first_block, tables, False)
        window_q = reduce_window(forward, freq_dev)
        mirrored = gather_columns(window_q, block_rows)
        adjoint = block_products(mirrored, response, ordered, first_block, tables, True)
        windowed = reduce_window(adjoint, freq_dev)
        current = (focus_init.astype(jnp.float32) + windowed.astype(jnp.float32)).astype(
            jnp.bfloat16
        )
    return (current, window_q)


def solution(mesh):
    return jax.shard_map(
        shards,
        mesh=mesh,
        in_specs=(
            P("freq", None, "rblk", None, None, None),
            P(),
            P("freq", None, None, "rblk"),
            P(None, "rblk"),
        ),
        out_specs=(P("freq", None, None, "rblk"), P("freq", None, None, "rblk")),
        check_vma=False,
    )
```

```python
import math

import jax
import jax.numpy as jnp
from jax import lax
from jax.experimental import pallas as pl
from jax.experimental.pallas import tpu as pltpu
from jax.sharding import PartitionSpec as P

NT = 4096
FBASE = 256
ITERS = 1
BLOCK = 128
NBUF = 5


def chunk_width(aper_w):
    for width in range(min(8, aper_w), 0, -1):
        if aper_w % width == 0:
            return width
    return 1


def live_counts(aperture, first_block, blk_dev):
    rows = lax.dynamic_slice_in_dim(aperture, first_block, blk_dev, 0)
    live = jnp.sum((rows >= 0).astype(jnp.int32), axis=1)
    return first_block.astype(jnp.int32).reshape(1), live


def block_products(gathered, response, aperture, first_block, tables, conjugate):
    freq_dev, unused, blk_dev, aper_w, block_rows, block_cols = response.shape
    rows_g = gathered.shape[2]
    chunk = chunk_width(aper_w)
    per_blk = aper_w // chunk
    meta, live = live_counts(aperture, first_block, blk_dev)
    flat_aperture = aperture.reshape(-1)
    focal = rows_g // 2
    freq_all = tables[0].shape[0] - freq_dev + 1
    scale = 1.0 / NT

    def kernel(aper_ref, meta_ref, live_ref, resp_hbm, g_ref,
               near_re_ref, near_im_ref, far_re_ref, far_im_ref, out_ref, buf, sem, pcat, acc,
               blk_ref, chk_ref):
        first = meta_ref[0]
        total = jnp.int32(0)
        for b in range(blk_dev):
            chunk_count = (live_ref[b] + chunk - 1) // chunk

            def fill(c, carry, b=b, base=total):
                blk_ref[base + c] = b
                chk_ref[base + c] = c
                return carry

            lax.fori_loop(0, chunk_count, fill, 0)
            total = total + chunk_count
        acc[...] = jnp.zeros(acc.shape, jnp.float32)

        def copies(entry, slot):
            b = blk_ref[entry]
            c = chk_ref[entry]
            return [
                pltpu.make_async_copy(
                    resp_hbm.at[:, :, b, c * chunk + t],
                    buf.at[slot, :, :, :, pl.ds(t * block_cols, block_cols)],
                    sem.at[slot, t],
                )
                for t in range(chunk)
            ]

        for slot in range(NBUF):
            @pl.when(slot < total)
            def _():
                for copy in copies(slot, slot):
                    copy.start()

        def body(entry, carry):
            slot = entry % NBUF
            b = blk_ref[entry]
            c = chk_ref[entry]
            count = live_ref[b]
            row = first + b
            for f in range(freq_dev):
                for t in range(chunk):
                    j = c * chunk + t
                    src = jnp.maximum(aper_ref[row * aper_w + j], 0)
                    piece = g_ref[src, f]
                    pcat[f, :, pl.ds(t * block_cols, block_cols)] = jnp.where(
                        j < count, piece, jnp.zeros_like(piece)
                    )
            for copy in copies(entry, slot):
                copy.wait()
            for f in range(freq_dev):
                tiles = buf[slot, f].reshape(2 * block_rows, chunk * block_cols)
                acc[b, f] += lax.dot_general(
                    tiles, pcat[f], (((1,), (1,)), ((), ())),
                    preferred_element_type=jnp.float32,
                )

            @pl.when(entry + NBUF < total)
            def _():
                for copy in copies(entry + NBUF, slot):
                    copy.start()

            return carry

        lax.fori_loop(0, total, body, 0)

        for b in range(blk_dev):
            cols = pl.ds(b * block_rows, block_rows)
            parts = []
            for f in range(freq_dev):
                v = acc[b, f].T
                p00 = v[0:focal, 0:block_rows]
                p01 = v[0:focal, block_rows:]
                p10 = v[focal:, 0:block_rows]
                p11 = v[focal:, block_rows:]
                if conjugate:
                    real_part = p00 + p11
                    imag_part = p10 - p01
                else:
                    real_part = p00 - p11
                    imag_part = p10 + p01
                parts.append((
                    real_part.astype(jnp.bfloat16).astype(jnp.float32),
                    imag_part.astype(jnp.bfloat16).astype(jnp.float32),
                ))
            for l in range(freq_all):
                new_real = None
                new_imag = None
                for f, (real_in, imag_in) in enumerate(parts):
                    near_at = f - l + freq_all - 1
                    far_at = f + l
                    rows = pl.ds(b * focal, focal)
                    near_re = near_re_ref[near_at, rows, :]
                    near_im = near_im_ref[near_at, rows, :]
                    far_re = far_re_ref[far_at, rows, :]
                    far_im = far_im_ref[far_at, rows, :]
                    term_real = real_in * (near_re + far_re) + imag_in * (far_im - near_im)
                    term_imag = real_in * (near_im + far_im) + imag_in * (near_re - far_re)
                    new_real = term_real if new_real is None else new_real + term_real
                    new_imag = term_imag if new_imag is None else new_imag + term_imag
                out_ref[l, 0, :, cols] = new_real * scale
                out_ref[l, 1, :, cols] = new_imag * scale

    smem = pl.BlockSpec(memory_space=pltpu.SMEM)
    vmem = pl.BlockSpec(memory_space=pltpu.VMEM)
    return pl.pallas_call(
        kernel,
        out_shape=jax.ShapeDtypeStruct(
            (freq_all, 2, focal, blk_dev * block_rows), jnp.float32
        ),
        in_specs=[smem] * 3 + [pl.BlockSpec(memory_space=pl.ANY)] + [vmem] * 5,
        out_specs=vmem,
        scratch_shapes=[
            pltpu.VMEM((NBUF, freq_dev, 2, block_rows, chunk * block_cols), response.dtype),
            pltpu.SemaphoreType.DMA((NBUF, chunk)),
            pltpu.VMEM((freq_dev, rows_g, chunk * block_cols), response.dtype),
            pltpu.VMEM((blk_dev, freq_dev, 2 * block_rows, rows_g), jnp.float32),
            pltpu.SMEM((blk_dev * per_blk,), jnp.int32),
            pltpu.SMEM((blk_dev * per_blk,), jnp.int32),
        ],
    )(flat_aperture, meta, live, response, gathered, *tables)


def gather_columns(spectra, block_rows):
    freq_dev, unused, focal, traces = spectra.shape
    blk_dev = traces // block_rows
    local = spectra.reshape(freq_dev, 2 * focal, blk_dev, block_rows)
    local = jnp.transpose(local, (2, 0, 1, 3))
    count = lax.axis_size("rblk")
    if count & (count - 1):
        return lax.all_gather(local, "rblk", axis=0, tiled=True)
    step = count // 2
    while step >= 1:
        pairs = [(i, i ^ step) for i in range(count)]
        local = jnp.concatenate([local, lax.ppermute(local, "rblk", pairs)], axis=0)
        step //= 2
    return local


def arrival_order(aperture, blk_dev):
    count = lax.axis_size("rblk")
    if count & (count - 1):
        return aperture
    me = lax.axis_index("rblk")
    partner = jnp.bitwise_xor(me, aperture // blk_dev)
    place = jnp.zeros_like(partner)
    bits = count.bit_length() - 1
    for bit in range(bits):
        place = place + ((partner >> (bits - 1 - bit)) & 1) * (1 << bit)
    return jnp.where(aperture >= 0, place * blk_dev + aperture % blk_dev, aperture)


def dirichlet(offsets, limits):
    span = 2 * NT
    full_turn = (limits * offsets) % span
    half_turn = ((limits - 1) * offsets) % span
    base_turn = offsets % span
    is_zero = (offsets % NT) == 0
    denom = jnp.where(
        is_zero, jnp.float32(1.0), jnp.sin(jnp.float32(math.pi) * base_turn.astype(jnp.float32) / NT)
    )
    ratio = jnp.where(
        is_zero,
        limits.astype(jnp.float32),
        jnp.sin(jnp.float32(math.pi) * full_turn.astype(jnp.float32) / NT) / denom,
    )
    angle = jnp.float32(math.pi) * half_turn.astype(jnp.float32) / NT
    return ratio * jnp.cos(angle), ratio * jnp.sin(angle)


def window_tables(arrival, freq_dev, freq_all):
    first = lax.axis_index("freq") * freq_dev
    steps = jnp.arange(freq_dev + freq_all - 1, dtype=jnp.int32)
    focal, traces = arrival.shape
    blocks = traces // BLOCK
    dense = jnp.transpose(arrival.reshape(focal, blocks, BLOCK), (1, 0, 2))
    limits = dense.reshape(blocks * focal, BLOCK)[None]
    near_offsets = first - (freq_all - 1) + steps
    far_offsets = -(2 * FBASE + first + steps)
    near_re, near_im = dirichlet(near_offsets[:, None, None], limits)
    far_re, far_im = dirichlet(far_offsets[:, None, None], limits)
    return near_re, near_im, far_re, far_im


def reduce_window(partial, freq_dev):
    count = lax.axis_size("freq")
    me = lax.axis_index("freq")
    summed = lax.dynamic_slice_in_dim(partial, me * freq_dev, freq_dev, 0)
    for shift in range(1, count):
        target = (me + shift) % count
        outgoing = lax.dynamic_slice_in_dim(partial, target * freq_dev, freq_dev, 0)
        pairs = [(i, (i + shift) % count) for i in range(count)]
        summed = summed + lax.ppermute(outgoing, "freq", pairs)
    return summed.astype(jnp.bfloat16)


def shards(response, aperture, focus_init, arrival):
    freq_dev = response.shape[0]
    blk_dev = response.shape[2]
    block_rows = response.shape[4]
    freq_all = freq_dev * lax.axis_size("freq")
    first_block = lax.axis_index("rblk") * blk_dev
    tables = window_tables(arrival, freq_dev, freq_all)
    ordered = arrival_order(aperture, blk_dev)
    current = focus_init
    window_q = focus_init
    for iteration in range(ITERS):
        gathered = gather_columns(current, block_rows)
        forward = block_products(gathered, response, ordered, first_block, tables, False)
        window_q = reduce_window(forward, freq_dev)
        mirrored = gather_columns(window_q, block_rows)
        adjoint = block_products(mirrored, response, ordered, first_block, tables, True)
        windowed = reduce_window(adjoint, freq_dev)
        current = (focus_init.astype(jnp.float32) + windowed.astype(jnp.float32)).astype(
            jnp.bfloat16
        )
    return (current, window_q)


def solution(mesh):
    return jax.shard_map(
        shards,
        mesh=mesh,
        in_specs=(
            P("freq", None, "rblk", None, None, None),
            P(),
            P("freq", None, None, "rblk"),
            P(None, "rblk"),
        ),
        out_specs=(P("freq", None, None, "rblk"), P("freq", None, None, "rblk")),
        check_vma=False,
    )
```

```python
import math

import jax
import jax.numpy as jnp
from jax import lax
from jax.experimental import pallas as pl
from jax.experimental.pallas import tpu as pltpu
from jax.sharding import PartitionSpec as P

NT = 4096
FBASE = 256
ITERS = 1
BLOCK = 128
NBUF = 5


def chunk_width(aper_w):
    for width in range(min(8, aper_w), 0, -1):
        if aper_w % width == 0:
            return width
    return 1


def live_counts(aperture, first_block, blk_dev):
    rows = lax.dynamic_slice_in_dim(aperture, first_block, blk_dev, 0)
    live = jnp.sum((rows >= 0).astype(jnp.int32), axis=1)
    return first_block.astype(jnp.int32).reshape(1), live


def block_products(gathered, response, aperture, first_block, tables, conjugate):
    freq_dev, unused, blk_dev, aper_w, block_rows, block_cols = response.shape
    rows_all = gathered.shape[1]
    rows_g = rows_all // freq_dev
    chunk = chunk_width(aper_w)
    per_blk = aper_w // chunk
    meta, live = live_counts(aperture, first_block, blk_dev)
    flat_aperture = aperture.reshape(-1)
    focal = rows_g // 2
    freq_all = tables[0].shape[0] - freq_dev + 1
    scale = 1.0 / NT

    def kernel(aper_ref, meta_ref, live_ref, resp_hbm, g_ref,
               near_re_ref, near_im_ref, far_re_ref, far_im_ref, out_ref, buf, sem, pcat, acc,
               blk_ref, chk_ref):
        first = meta_ref[0]
        total = jnp.int32(0)
        for b in range(blk_dev):
            chunk_count = (live_ref[b] + chunk - 1) // chunk

            def fill(c, carry, b=b, base=total):
                blk_ref[base + c] = b
                chk_ref[base + c] = c
                return carry

            lax.fori_loop(0, chunk_count, fill, 0)
            total = total + chunk_count
        acc[...] = jnp.zeros(acc.shape, jnp.float32)

        def copies(entry, slot):
            b = blk_ref[entry]
            c = chk_ref[entry]
            return [
                pltpu.make_async_copy(
                    resp_hbm.at[:, :, b, c * chunk + t],
                    buf.at[slot, :, :, :, pl.ds(t * block_cols, block_cols)],
                    sem.at[slot, t],
                )
                for t in range(chunk)
            ]

        for slot in range(NBUF):
            @pl.when(slot < total)
            def _():
                for copy in copies(slot, slot):
                    copy.start()

        def body(entry, carry):
            slot = entry % NBUF
            b = blk_ref[entry]
            c = chk_ref[entry]
            count = live_ref[b]
            row = first + b
            for t in range(chunk):
                j = c * chunk + t
                src = jnp.maximum(aper_ref[row * aper_w + j], 0)
                piece = g_ref[src]
                pcat[:, pl.ds(t * block_cols, block_cols)] = jnp.where(
                    j < count, piece, jnp.zeros_like(piece)
                )
            for copy in copies(entry, slot):
                copy.wait()
            for f in range(freq_dev):
                tiles = buf[slot, f].reshape(2 * block_rows, chunk * block_cols)
                acc[b, f] += lax.dot_general(
                    tiles, pcat[...], (((1,), (1,)), ((), ())),
                    preferred_element_type=jnp.float32,
                )

            @pl.when(entry + NBUF < total)
            def _():
                for copy in copies(entry + NBUF, slot):
                    copy.start()

            return carry

        lax.fori_loop(0, total, body, 0)

        for b in range(blk_dev):
            cols = pl.ds(b * block_rows, block_rows)
            parts = []
            for f in range(freq_dev):
                v = acc[b, f].T[f * rows_g:(f + 1) * rows_g]
                p00 = v[0:focal, 0:block_rows]
                p01 = v[0:focal, block_rows:]
                p10 = v[focal:, 0:block_rows]
                p11 = v[focal:, block_rows:]
                if conjugate:
                    real_part = p00 + p11
                    imag_part = p10 - p01
                else:
                    real_part = p00 - p11
                    imag_part = p10 + p01
                parts.append((
                    real_part.astype(jnp.bfloat16).astype(jnp.float32),
                    imag_part.astype(jnp.bfloat16).astype(jnp.float32),
                ))
            for l in range(freq_all):
                new_real = None
                new_imag = None
                for f, (real_in, imag_in) in enumerate(parts):
                    near_at = f - l + freq_all - 1
                    far_at = f + l
                    rows = pl.ds(b * focal, focal)
                    near_re = near_re_ref[near_at, rows, :]
                    near_im = near_im_ref[near_at, rows, :]
                    far_re = far_re_ref[far_at, rows, :]
                    far_im = far_im_ref[far_at, rows, :]
                    term_real = real_in * (near_re + far_re) + imag_in * (far_im - near_im)
                    term_imag = real_in * (near_im + far_im) + imag_in * (near_re - far_re)
                    new_real = term_real if new_real is None else new_real + term_real
                    new_imag = term_imag if new_imag is None else new_imag + term_imag
                out_ref[l, 0, :, cols] = new_real * scale
                out_ref[l, 1, :, cols] = new_imag * scale

    smem = pl.BlockSpec(memory_space=pltpu.SMEM)
    vmem = pl.BlockSpec(memory_space=pltpu.VMEM)
    return pl.pallas_call(
        kernel,
        out_shape=jax.ShapeDtypeStruct(
            (freq_all, 2, focal, blk_dev * block_rows), jnp.float32
        ),
        in_specs=[smem] * 3 + [pl.BlockSpec(memory_space=pl.ANY)] + [vmem] * 5,
        out_specs=vmem,
        scratch_shapes=[
            pltpu.VMEM((NBUF, freq_dev, 2, block_rows, chunk * block_cols), response.dtype),
            pltpu.SemaphoreType.DMA((NBUF, chunk)),
            pltpu.VMEM((rows_all, chunk * block_cols), response.dtype),
            pltpu.VMEM((blk_dev, freq_dev, 2 * block_rows, rows_all), jnp.float32),
            pltpu.SMEM((blk_dev * per_blk,), jnp.int32),
            pltpu.SMEM((blk_dev * per_blk,), jnp.int32),
        ],
    )(flat_aperture, meta, live, response, gathered, *tables)


def gather_columns(spectra, block_rows):
    freq_dev, unused, focal, traces = spectra.shape
    blk_dev = traces // block_rows
    local = spectra.reshape(freq_dev * 2 * focal, blk_dev, block_rows)
    local = jnp.transpose(local, (1, 0, 2))
    count = lax.axis_size("rblk")
    if count & (count - 1):
        return lax.all_gather(local, "rblk", axis=0, tiled=True)
    step = count // 2
    while step >= 1:
        pairs = [(i, i ^ step) for i in range(count)]
        local = jnp.concatenate([local, lax.ppermute(local, "rblk", pairs)], axis=0)
        step //= 2
    return local


def arrival_order(aperture, blk_dev):
    count = lax.axis_size("rblk")
    if count & (count - 1):
        return aperture
    me = lax.axis_index("rblk")
    partner = jnp.bitwise_xor(me, aperture // blk_dev)
    place = jnp.zeros_like(partner)
    bits = count.bit_length() - 1
    for bit in range(bits):
        place = place + ((partner >> (bits - 1 - bit)) & 1) * (1 << bit)
    return jnp.where(aperture >= 0, place * blk_dev + aperture % blk_dev, aperture)


def dirichlet(offsets, limits):
    span = 2 * NT
    full_turn = (limits * offsets) % span
    half_turn = ((limits - 1) * offsets) % span
    base_turn = offsets % span
    is_zero = (offsets % NT) == 0
    denom = jnp.where(
        is_zero, jnp.float32(1.0), jnp.sin(jnp.float32(math.pi) * base_turn.astype(jnp.float32) / NT)
    )
    ratio = jnp.where(
        is_zero,
        limits.astype(jnp.float32),
        jnp.sin(jnp.float32(math.pi) * full_turn.astype(jnp.float32) / NT) / denom,
    )
    angle = jnp.float32(math.pi) * half_turn.astype(jnp.float32) / NT
    return ratio * jnp.cos(angle), ratio * jnp.sin(angle)


def window_tables(arrival, freq_dev, freq_all):
    first = lax.axis_index("freq") * freq_dev
    steps = jnp.arange(freq_dev + freq_all - 1, dtype=jnp.int32)
    focal, traces = arrival.shape
    blocks = traces // BLOCK
    dense = jnp.transpose(arrival.reshape(focal, blocks, BLOCK), (1, 0, 2))
    limits = dense.reshape(blocks * focal, BLOCK)[None]
    near_offsets = first - (freq_all - 1) + steps
    far_offsets = -(2 * FBASE + first + steps)
    near_re, near_im = dirichlet(near_offsets[:, None, None], limits)
    far_re, far_im = dirichlet(far_offsets[:, None, None], limits)
    return near_re, near_im, far_re, far_im


def reduce_window(partial, freq_dev):
    count = lax.axis_size("freq")
    me = lax.axis_index("freq")
    summed = lax.dynamic_slice_in_dim(partial, me * freq_dev, freq_dev, 0)
    for shift in range(1, count):
        target = (me + shift) % count
        outgoing = lax.dynamic_slice_in_dim(partial, target * freq_dev, freq_dev, 0)
        pairs = [(i, (i + shift) % count) for i in range(count)]
        summed = summed + lax.ppermute(outgoing, "freq", pairs)
    return summed.astype(jnp.bfloat16)


def shards(response, aperture, focus_init, arrival):
    freq_dev = response.shape[0]
    blk_dev = response.shape[2]
    block_rows = response.shape[4]
    freq_all = freq_dev * lax.axis_size("freq")
    first_block = lax.axis_index("rblk") * blk_dev
    tables = window_tables(arrival, freq_dev, freq_all)
    ordered = arrival_order(aperture, blk_dev)
    current = focus_init
    window_q = focus_init
    for iteration in range(ITERS):
        gathered = gather_columns(current, block_rows)
        forward = block_products(gathered, response, ordered, first_block, tables, False)
        window_q = reduce_window(forward, freq_dev)
        mirrored = gather_columns(window_q, block_rows)
        adjoint = block_products(mirrored, response, ordered, first_block, tables, True)
        windowed = reduce_window(adjoint, freq_dev)
        current = (focus_init.astype(jnp.float32) + windowed.astype(jnp.float32)).astype(
            jnp.bfloat16
        )
    return (current, window_q)


def solution(mesh):
    return jax.shard_map(
        shards,
        mesh=mesh,
        in_specs=(
            P("freq", None, "rblk", None, None, None),
            P(),
            P("freq", None, None, "rblk"),
            P(None, "rblk"),
        ),
        out_specs=(P("freq", None, None, "rblk"), P("freq", None, None, "rblk")),
        check_vma=False,
    )
```

```python
import math

import jax
import jax.numpy as jnp
from jax import lax
from jax.experimental import pallas as pl
from jax.experimental.pallas import tpu as pltpu
from jax.sharding import PartitionSpec as P

NT = 4096
FBASE = 256
ITERS = 1
BLOCK = 128
NBUF = 5


def chunk_width(aper_w):
    for width in range(min(8, aper_w), 0, -1):
        if aper_w % width == 0:
            return width
    return 1


def live_counts(aperture, first_block, blk_dev):
    rows = lax.dynamic_slice_in_dim(aperture, first_block, blk_dev, 0)
    live = jnp.sum((rows >= 0).astype(jnp.int32), axis=1)
    return first_block.astype(jnp.int32).reshape(1), live


def block_products(gathered, response, aperture, first_block, tables, conjugate):
    freq_dev, unused, blk_dev, aper_w, block_rows, block_cols = response.shape
    rows_all = gathered.shape[1]
    rows_g = rows_all // freq_dev
    chunk = chunk_width(aper_w)
    per_blk = aper_w // chunk
    meta, live = live_counts(aperture, first_block, blk_dev)
    flat_aperture = aperture.reshape(-1)
    focal = rows_g // 2
    freq_all = tables[0].shape[0] - freq_dev + 1
    scale = 1.0 / NT

    def kernel(aper_ref, meta_ref, live_ref, resp_hbm, g_ref,
               near_re_ref, near_im_ref, far_re_ref, far_im_ref, out_ref, buf, sem, pcat, acc,
               blk_ref, chk_ref):
        first = meta_ref[0]
        total = jnp.int32(0)
        for b in range(blk_dev):
            chunk_count = (live_ref[b] + chunk - 1) // chunk

            def fill(c, carry, b=b, base=total):
                blk_ref[base + c] = b
                chk_ref[base + c] = c
                return carry

            lax.fori_loop(0, chunk_count, fill, 0)
            total = total + chunk_count
        acc[...] = jnp.zeros(acc.shape, jnp.float32)

        def copies(entry, slot):
            b = blk_ref[entry]
            c = chk_ref[entry]
            return [
                pltpu.make_async_copy(
                    resp_hbm.at[:, :, b, c * chunk + t],
                    buf.at[slot, :, :, :, pl.ds(t * block_cols, block_cols)],
                    sem.at[slot, t],
                )
                for t in range(chunk)
            ]

        for slot in range(NBUF):
            @pl.when(slot < total)
            def _():
                for copy in copies(slot, slot):
                    copy.start()

        def body(entry, carry):
            slot = entry % NBUF
            b = blk_ref[entry]
            c = chk_ref[entry]
            count = live_ref[b]
            row = first + b
            for t in range(chunk):
                j = c * chunk + t
                src = jnp.maximum(aper_ref[row * aper_w + j], 0)
                piece = g_ref[src]
                pcat[:, pl.ds(t * block_cols, block_cols)] = jnp.where(
                    j < count, piece, jnp.zeros_like(piece)
                )
            for copy in copies(entry, slot):
                copy.wait()
            for f in range(freq_dev):
                tiles = buf[slot, f].reshape(2 * block_rows, chunk * block_cols)
                acc[b, f] += lax.dot_general(
                    tiles, pcat[...], (((1,), (1,)), ((), ())),
                    preferred_element_type=jnp.float32,
                )

            @pl.when(entry + NBUF < total)
            def _():
                for copy in copies(entry + NBUF, slot):
                    copy.start()

            return carry

        lax.fori_loop(0, total, body, 0)

        group = 2 if blk_dev % 2 == 0 else 1
        for b0 in range(0, blk_dev, group):
            parts = []
            for f in range(freq_dev):
                reals = []
                imags = []
                for b in range(b0, b0 + group):
                    v = acc[b, f].T[f * rows_g:(f + 1) * rows_g]
                    p00 = v[0:focal, 0:block_rows]
                    p01 = v[0:focal, block_rows:]
                    p10 = v[focal:, 0:block_rows]
                    p11 = v[focal:, block_rows:]
                    if conjugate:
                        reals.append(p00 + p11)
                        imags.append(p10 - p01)
                    else:
                        reals.append(p00 - p11)
                        imags.append(p10 + p01)
                real_part = jnp.concatenate(reals, axis=0) if group > 1 else reals[0]
                imag_part = jnp.concatenate(imags, axis=0) if group > 1 else imags[0]
                parts.append((
                    real_part.astype(jnp.bfloat16).astype(jnp.float32),
                    imag_part.astype(jnp.bfloat16).astype(jnp.float32),
                ))
            rows = pl.ds(b0 * focal, group * focal)
            for l in range(freq_all):
                new_real = None
                new_imag = None
                for f, (real_in, imag_in) in enumerate(parts):
                    near_at = f - l + freq_all - 1
                    far_at = f + l
                    near_re = near_re_ref[near_at, rows, :]
                    near_im = near_im_ref[near_at, rows, :]
                    far_re = far_re_ref[far_at, rows, :]
                    far_im = far_im_ref[far_at, rows, :]
                    term_real = real_in * (near_re + far_re) + imag_in * (far_im - near_im)
                    term_imag = real_in * (near_im + far_im) + imag_in * (near_re - far_re)
                    new_real = term_real if new_real is None else new_real + term_real
                    new_imag = term_imag if new_imag is None else new_imag + term_imag
                new_real = new_real * scale
                new_imag = new_imag * scale
                for k in range(group):
                    cols = pl.ds((b0 + k) * block_rows, block_rows)
                    out_ref[l, 0, :, cols] = new_real[k * focal:(k + 1) * focal]
                    out_ref[l, 1, :, cols] = new_imag[k * focal:(k + 1) * focal]

    smem = pl.BlockSpec(memory_space=pltpu.SMEM)
    vmem = pl.BlockSpec(memory_space=pltpu.VMEM)
    return pl.pallas_call(
        kernel,
        out_shape=jax.ShapeDtypeStruct(
            (freq_all, 2, focal, blk_dev * block_rows), jnp.float32
        ),
        in_specs=[smem] * 3 + [pl.BlockSpec(memory_space=pl.ANY)] + [vmem] * 5,
        out_specs=vmem,
        scratch_shapes=[
            pltpu.VMEM((NBUF, freq_dev, 2, block_rows, chunk * block_cols), response.dtype),
            pltpu.SemaphoreType.DMA((NBUF, chunk)),
            pltpu.VMEM((rows_all, chunk * block_cols), response.dtype),
            pltpu.VMEM((blk_dev, freq_dev, 2 * block_rows, rows_all), jnp.float32),
            pltpu.SMEM((blk_dev * per_blk,), jnp.int32),
            pltpu.SMEM((blk_dev * per_blk,), jnp.int32),
        ],
    )(flat_aperture, meta, live, response, gathered, *tables)


def gather_columns(spectra, block_rows):
    freq_dev, unused, focal, traces = spectra.shape
    blk_dev = traces // block_rows
    local = spectra.reshape(freq_dev * 2 * focal, blk_dev, block_rows)
    local = jnp.transpose(local, (1, 0, 2))
    count = lax.axis_size("rblk")
    if count & (count - 1):
        return lax.all_gather(local, "rblk", axis=0, tiled=True)
    step = count // 2
    while step >= 1:
        pairs = [(i, i ^ step) for i in range(count)]
        local = jnp.concatenate([local, lax.ppermute(local, "rblk", pairs)], axis=0)
        step //= 2
    return local


def arrival_order(aperture, blk_dev):
    count = lax.axis_size("rblk")
    if count & (count - 1):
        return aperture
    me = lax.axis_index("rblk")
    partner = jnp.bitwise_xor(me, aperture // blk_dev)
    place = jnp.zeros_like(partner)
    bits = count.bit_length() - 1
    for bit in range(bits):
        place = place + ((partner >> (bits - 1 - bit)) & 1) * (1 << bit)
    return jnp.where(aperture >= 0, place * blk_dev + aperture % blk_dev, aperture)


def dirichlet(offsets, limits):
    span = 2 * NT
    full_turn = (limits * offsets) % span
    half_turn = ((limits - 1) * offsets) % span
    base_turn = offsets % span
    is_zero = (offsets % NT) == 0
    denom = jnp.where(
        is_zero, jnp.float32(1.0), jnp.sin(jnp.float32(math.pi) * base_turn.astype(jnp.float32) / NT)
    )
    ratio = jnp.where(
        is_zero,
        limits.astype(jnp.float32),
        jnp.sin(jnp.float32(math.pi) * full_turn.astype(jnp.float32) / NT) / denom,
    )
    angle = jnp.float32(math.pi) * half_turn.astype(jnp.float32) / NT
    return ratio * jnp.cos(angle), ratio * jnp.sin(angle)


def window_tables(arrival, freq_dev, freq_all):
    first = lax.axis_index("freq") * freq_dev
    steps = jnp.arange(freq_dev + freq_all - 1, dtype=jnp.int32)
    focal, traces = arrival.shape
    blocks = traces // BLOCK
    dense = jnp.transpose(arrival.reshape(focal, blocks, BLOCK), (1, 0, 2))
    limits = dense.reshape(blocks * focal, BLOCK)[None]
    near_offsets = first - (freq_all - 1) + steps
    far_offsets = -(2 * FBASE + first + steps)
    near_re, near_im = dirichlet(near_offsets[:, None, None], limits)
    far_re, far_im = dirichlet(far_offsets[:, None, None], limits)
    return near_re, near_im, far_re, far_im


def reduce_window(partial, freq_dev):
    count = lax.axis_size("freq")
    me = lax.axis_index("freq")
    summed = lax.dynamic_slice_in_dim(partial, me * freq_dev, freq_dev, 0)
    for shift in range(1, count):
        target = (me + shift) % count
        outgoing = lax.dynamic_slice_in_dim(partial, target * freq_dev, freq_dev, 0)
        pairs = [(i, (i + shift) % count) for i in range(count)]
        summed = summed + lax.ppermute(outgoing, "freq", pairs)
    return summed.astype(jnp.bfloat16)


def shards(response, aperture, focus_init, arrival):
    freq_dev = response.shape[0]
    blk_dev = response.shape[2]
    block_rows = response.shape[4]
    freq_all = freq_dev * lax.axis_size("freq")
    first_block = lax.axis_index("rblk") * blk_dev
    tables = window_tables(arrival, freq_dev, freq_all)
    ordered = arrival_order(aperture, blk_dev)
    current = focus_init
    window_q = focus_init
    for iteration in range(ITERS):
        gathered = gather_columns(current, block_rows)
        forward = block_products(gathered, response, ordered, first_block, tables, False)
        window_q = reduce_window(forward, freq_dev)
        mirrored = gather_columns(window_q, block_rows)
        adjoint = block_products(mirrored, response, ordered, first_block, tables, True)
        windowed = reduce_window(adjoint, freq_dev)
        current = (focus_init.astype(jnp.float32) + windowed.astype(jnp.float32)).astype(
            jnp.bfloat16
        )
    return (current, window_q)


def solution(mesh):
    return jax.shard_map(
        shards,
        mesh=mesh,
        in_specs=(
            P("freq", None, "rblk", None, None, None),
            P(),
            P("freq", None, None, "rblk"),
            P(None, "rblk"),
        ),
        out_specs=(P("freq", None, None, "rblk"), P("freq", None, None, "rblk")),
        check_vma=False,
    )
```
